768 devices in a mesh: tm: 8 (over x, core), height: 96 (over z, y).
Axes of the slice: x: 4, y: 8, z: 12, core: 2. Of those that a mesh axis runs over, the one named last changes fastest.
Arguments:
- clip: bfloat16 [16, 384, 64, 256], P('tm', 'height'), may hold values from -6 to 6
- cotangent: bfloat16 [16, 384, 64, 256], P('tm', 'height'), may hold values from -6 to 6
- spatial_weight: bfloat16 [3, 3, 256, 256], replicated, may hold values from -0.125 to 0.125
- temporal_weight: bfloat16 [3, 256, 256], replicated, may hold values from -0.21875 to 0.21875
Outputs:
- output: bfloat16 [16, 384, 64, 256], P('tm', 'height')
- grad_clip: bfloat16 [16, 384, 64, 256], P('tm', 'height')
- grad_spatial: float32 [589824], P(('tm', 'height'))
- grad_temporal: float32 [196608], P(('tm', 'height'))
The draws below stay inside these ranges and needn't reach their ends.
All inputs are finite; a program needn't handle non-finite values.
Results may differ from the reference program's by a relative error of at most 0.0049.
Values may be sent and summed in bfloat16 or wider, within the bound.
No kernel may reach another device: no remote copies, remote signals or barrier semaphores. Data moves between devices by JAX's collectives and lax.ppermute only.
A program may use at most 32 MiB of HBM per device.

```python
import math
import jax
import jax.numpy as jnp
from jax import lax

C = 256
W = 64
FRAMES = 16
HEIGHT = 384


def levels(own_key, dims, pieces, low, high):
    gain, own = 1.0, jax.random.fold_in(own_key, 6)
    for position, shards_of in pieces:
        heights = jnp.exp(jax.random.uniform(jax.random.fold_in(own, position), (shards_of,), jnp.float32, low / len(pieces), high / len(pieces)))
        gain = gain * jnp.repeat(heights, dims[position] // shards_of).reshape([-1 if axis == position else 1 for axis in range(len(dims))])
    return gain


def scatter_about(rng, shape, deviation, limit, shards=(), kind=jnp.bfloat16):
    values = jax.random.normal(rng, shape, jnp.float32) * deviation
    if len(shards) > 0:
        values = levels(rng, shape, shards, -0.22, 0.18) * values
    return jnp.clip(values, min=-limit, max=limit).astype(kind)


def setup_inputs(seed: int = 0) -> dict:
    key_list = jax.random.split(jax.random.key(seed), 5)
    clip = scatter_about(key_list[0], (FRAMES, HEIGHT, W, C), 1.0, 6.0, ((0, 8), (1, 96)))
    cotangent = scatter_about(key_list[1], (FRAMES, HEIGHT, W, C), 1.0, 6.0, ((0, 8), (1, 96)))
    spatial_weight = scatter_about(key_list[2], (3, 3, C, C), (9 * C) ** -0.5, 0.125)
    temporal_weight = scatter_about(key_list[3], (3, C, C), (3 * C) ** -0.5, 0.21875)
    return {"clip": clip, "cotangent": cotangent, "spatial_weight": spatial_weight, "temporal_weight": temporal_weight}


EPSILON = 1e-06

def activate(values):
    scale_inv = lax.rsqrt(lax.optimization_barrier(jnp.mean(values * values, axis=-1, keepdims=True)) + EPSILON)
    return jax.nn.silu(values * scale_inv)

def flat_dot(left, weight):
    keep_shape = left.shape[:-1]
    result = jnp.dot(left.reshape(-1, left.shape[-1]), weight, preferred_element_type=jnp.float32)
    return result.reshape(keep_shape + (weight.shape[-1],))

def outer_sum(left, right):
    channels = left.shape[-1]
    return lax.dot_general(left.reshape(-1, channels), right.reshape(-1, channels), (((0,), (0,)), ((), ())), preferred_element_type=jnp.float32)

def reference(clip, cotangent, spatial_weight, temporal_weight):
    frame_count, row_count, col_count, channels = clip.shape
    clip_wide = clip.astype(jnp.float32)
    activated = activate(clip_wide).astype(jnp.bfloat16)
    padded = jnp.pad(activated, ((0, 0), (1, 1), (1, 1), (0, 0)))
    spatial = jnp.zeros(clip.shape, jnp.float32)
    for tap_row in range(3):
        for tap_col in range(3):
            spatial = spatial + flat_dot(padded[:, tap_row:tap_row + row_count, tap_col:tap_col + col_count], spatial_weight[tap_row, tap_col])
    middle = spatial.astype(jnp.bfloat16)
    history = jnp.pad(middle, ((2, 0), (0, 0), (0, 0), (0, 0)))
    temporal = jnp.zeros(clip.shape, jnp.float32)
    for time_lag in range(3):
        temporal = temporal + flat_dot(history[2 - time_lag:2 - time_lag + frame_count], temporal_weight[time_lag])
    output = (clip_wide + temporal).astype(jnp.bfloat16)
    future = jnp.pad(cotangent, ((0, 2), (0, 0), (0, 0), (0, 0)))
    grad_wide = jnp.zeros(clip.shape, jnp.float32)
    for time_lag in range(3):
        grad_wide = grad_wide + flat_dot(future[time_lag:time_lag + frame_count], temporal_weight[time_lag].T)
    grad_mid = grad_wide.astype(jnp.bfloat16)
    grad_temporal = jnp.stack([outer_sum(history[2 - time_lag:2 - time_lag + frame_count], cotangent) for time_lag in range(3)])
    terms = []
    for tap_row in range(3):
        for tap_col in range(3):
            terms.append(outer_sum(padded[:, tap_row:tap_row + row_count, tap_col:tap_col + col_count], grad_mid))
    grad_spatial = jnp.stack(terms)
    grad_pad = jnp.pad(grad_mid, ((0, 0), (1, 1), (1, 1), (0, 0)))
    grad_act = jnp.zeros(clip.shape, jnp.float32)
    for tap_row in range(3):
        for tap_col in range(3):
            grad_act = grad_act + flat_dot(grad_pad[:, 2 - tap_row:2 - tap_row + row_count, 2 - tap_col:2 - tap_col + col_count], spatial_weight[tap_row, tap_col].T)
    unused, pullback = jax.vjp(activate, clip_wide)
    grad_clip = (cotangent.astype(jnp.float32) + pullback(grad_act)[0]).astype(jnp.bfloat16)
    grad_scale = 1.0 / math.sqrt(frame_count * row_count * col_count)
    return (output, grad_clip, (grad_spatial * grad_scale).reshape(-1), (grad_temporal * grad_scale).reshape(-1))
```

```python
import math

import jax
import jax.numpy as jnp
from jax import lax
from jax.sharding import PartitionSpec as P

EPSILON = 1e-06


def extended(cells, sides, width):
    for axis, dim in sides:
        count = lax.axis_size(axis)
        ends = count - 1
        head = lax.slice_in_dim(cells, 0, width, axis=dim)
        tail = lax.slice_in_dim(cells, cells.shape[dim] - width, cells.shape[dim], axis=dim)
        cells = jnp.concatenate(
            [
                lax.ppermute(tail, axis, [(i, (i + 1) % count) for i in range(ends)]),
                cells,
                lax.ppermute(head, axis, [((i + 1) % count, i) for i in range(ends)]),
            ],
            axis=dim,
        )
    return cells


def shifted(block, axis, distance):
    devices = range(lax.axis_size(axis))
    route = [(i - distance, i) for i in devices if i - distance in devices]
    return lax.ppermute(block, axis, route)


def activate(values):
    scale_inv = lax.rsqrt(jnp.mean(values * values, axis=-1, keepdims=True) + EPSILON)
    return jax.nn.silu(values * scale_inv)


def flat_dot(left, weight):
    keep_shape = left.shape[:-1]
    result = jnp.dot(left.reshape(-1, left.shape[-1]), weight, preferred_element_type=jnp.float32)
    return result.reshape(keep_shape + (weight.shape[-1],))


def outer_sum(left, right):
    channels = left.shape[-1]
    return lax.dot_general(
        left.reshape(-1, channels),
        right.reshape(-1, channels),
        (((0,), (0,)), ((), ())),
        preferred_element_type=jnp.float32,
    )


def halving_scatter(block, axis):
    count = lax.axis_size(axis)
    index = lax.axis_index(axis)
    step = 1
    while count // step % 2 == 0:
        rest = block.shape[1:]
        pairs = block.reshape((block.shape[0] // 2, 2) + rest)
        mine = index // step % 2
        keep = lax.dynamic_index_in_dim(pairs, mine, axis=1, keepdims=False)
        send = lax.dynamic_index_in_dim(pairs, 1 - mine, axis=1, keepdims=False)
        route = [(i, i ^ step) for i in range(count)]
        block = keep + lax.ppermute(send, axis, route)
        step *= 2
    ways = count // step
    if ways > 1:
        group = index // step
        total = lax.dynamic_index_in_dim(block, group, axis=0, keepdims=True)
        for shift in range(1, ways):
            route = [(i, (i + shift * step) % count) for i in range(count)]
            row = lax.dynamic_index_in_dim(block, (group + shift) % ways, axis=0, keepdims=True)
            total = total + lax.ppermute(row, axis, route)
        block = total
    return block


def shards(clip, cotangent, spatial_weight, temporal_weight):
    frame_count, row_count, col_count, channels = clip.shape
    clip_wide = clip.astype(jnp.float32)
    activated = activate(clip_wide).astype(jnp.bfloat16)
    act_ext = extended(activated, (("height", 1),), 1)
    padded = jnp.pad(act_ext, ((0, 0), (0, 0), (1, 1), (0, 0)))
    spatial = jnp.zeros(clip.shape, jnp.float32)
    for tap_row in range(3):
        for tap_col in range(3):
            spatial = spatial + flat_dot(
                padded[:, tap_row : tap_row + row_count, tap_col : tap_col + col_count],
                spatial_weight[tap_row, tap_col],
            )
    middle = spatial.astype(jnp.bfloat16)
    earlier = shifted(middle, "tm", 1)
    history = jnp.concatenate([earlier, middle], axis=0)
    temporal = jnp.zeros(clip.shape, jnp.float32)
    for time_lag in range(3):
        temporal = temporal + flat_dot(
            history[2 - time_lag : 2 - time_lag + frame_count], temporal_weight[time_lag]
        )
    output = (clip_wide + temporal).astype(jnp.bfloat16)
    later = shifted(cotangent, "tm", -1)
    future = jnp.concatenate([cotangent, later], axis=0)
    grad_wide = jnp.zeros(clip.shape, jnp.float32)
    for time_lag in range(3):
        grad_wide = grad_wide + flat_dot(
            future[time_lag : time_lag + frame_count], temporal_weight[time_lag].T
        )
    grad_mid = grad_wide.astype(jnp.bfloat16)
    grad_temporal = jnp.stack(
        [
            outer_sum(history[2 - time_lag : 2 - time_lag + frame_count], cotangent)
            for time_lag in range(3)
        ]
    )
    grad_ext = extended(grad_mid, (("height", 1),), 1)
    grad_pad = jnp.pad(grad_ext, ((0, 0), (0, 0), (1, 1), (0, 0)))
    terms = []
    for tap_row in range(3):
        for tap_col in range(3):
            terms.append(
                outer_sum(
                    padded[:, tap_row : tap_row + row_count, tap_col : tap_col + col_count],
                    grad_mid,
                )
            )
    grad_spatial = jnp.stack(terms)
    grad_act = jnp.zeros(clip.shape, jnp.float32)
    for tap_row in range(3):
        for tap_col in range(3):
            grad_act = grad_act + flat_dot(
                grad_pad[
                    :, 2 - tap_row : 2 - tap_row + row_count, 2 - tap_col : 2 - tap_col + col_count
                ],
                spatial_weight[tap_row, tap_col].T,
            )
    unused, pullback = jax.vjp(activate, clip_wide)
    grad_clip = (cotangent.astype(jnp.float32) + pullback(grad_act)[0]).astype(jnp.bfloat16)
    time_shards = lax.axis_size("tm")
    row_shards = lax.axis_size("height")
    grad_scale = 1.0 / math.sqrt(frame_count * time_shards * row_count * row_shards * col_count)
    devices = time_shards * row_shards
    spatial_rows = grad_spatial.reshape(devices, -1)
    temporal_rows = grad_temporal.reshape(devices, -1)
    packed = jnp.concatenate([spatial_rows, temporal_rows], axis=1)
    packed = packed.reshape(time_shards, row_shards, packed.shape[-1])
    packed = halving_scatter(packed, "tm")[0]
    packed = halving_scatter(packed, "height")[0]
    packed = packed * grad_scale
    spatial_part = packed[: spatial_rows.shape[1]]
    temporal_part = packed[spatial_rows.shape[1] :]
    return (output, grad_clip, spatial_part, temporal_part)


def solution(mesh):
    return jax.shard_map(
        shards,
        mesh=mesh,
        in_specs=(P("tm", "height", None, None), P("tm", "height", None, None), P(), P()),
        out_specs=(
            P("tm", "height", None, None),
            P("tm", "height", None, None),
            P(("tm", "height")),
            P(("tm", "height")),
        ),
        check_vma=False,
    )
```

```python
import math

import jax
import jax.numpy as jnp
from jax import lax
from jax.sharding import PartitionSpec as P

EPSILON = 1e-06


def extended(cells, sides, width):
    for axis, dim in sides:
        count = lax.axis_size(axis)
        ends = count - 1
        head = lax.slice_in_dim(cells, 0, width, axis=dim)
        tail = lax.slice_in_dim(cells, cells.shape[dim] - width, cells.shape[dim], axis=dim)
        cells = jnp.concatenate(
            [
                lax.ppermute(tail, axis, [(i, (i + 1) % count) for i in range(ends)]),
                cells,
                lax.ppermute(head, axis, [((i + 1) % count, i) for i in range(ends)]),
            ],
            axis=dim,
        )
    return cells


def shifted(block, axis, distance):
    devices = range(lax.axis_size(axis))
    route = [(i - distance, i) for i in devices if i - distance in devices]
    return lax.ppermute(block, axis, route)


def activate(values):
    scale_inv = lax.rsqrt(jnp.mean(values * values, axis=-1, keepdims=True) + EPSILON)
    return jax.nn.silu(values * scale_inv)


def flat_dot(left, weight):
    keep_shape = left.shape[:-1]
    result = jnp.dot(left.reshape(-1, left.shape[-1]), weight, preferred_element_type=jnp.float32)
    return result.reshape(keep_shape + (weight.shape[-1],))


def outer_sum(left, right):
    channels = left.shape[-1]
    return lax.dot_general(
        left.reshape(-1, channels),
        right.reshape(-1, channels),
        (((0,), (0,)), ((), ())),
        preferred_element_type=jnp.float32,
    )


def halving_scatter(block, axis):
    count = lax.axis_size(axis)
    index = lax.axis_index(axis)
    step = 1
    while count // step % 2 == 0:
        rest = block.shape[1:]
        pairs = block.reshape((block.shape[0] // 2, 2) + rest)
        mine = index // step % 2
        keep = lax.dynamic_index_in_dim(pairs, mine, axis=1, keepdims=False)
        send = lax.dynamic_index_in_dim(pairs, 1 - mine, axis=1, keepdims=False)
        route = [(i, i ^ step) for i in range(count)]
        block = keep + lax.ppermute(send, axis, route)
        step *= 2
    ways = count // step
    if ways > 1:
        group = index // step
        total = lax.dynamic_index_in_dim(block, group, axis=0, keepdims=True)
        for shift in range(1, ways):
            route = [(i, (i + shift * step) % count) for i in range(count)]
            row = lax.dynamic_index_in_dim(block, (group + shift) % ways, axis=0, keepdims=True)
            total = total + lax.ppermute(row, axis, route)
        block = total
    return block


def shards(clip, cotangent, spatial_weight, temporal_weight):
    frame_count, row_count, col_count, channels = clip.shape
    clip_wide = clip.astype(jnp.float32)
    activated = activate(clip_wide).astype(jnp.bfloat16)
    act_ext = extended(activated, (("height", 1),), 1)
    padded = jnp.pad(act_ext, ((0, 0), (0, 0), (1, 1), (0, 0)))
    spatial = jnp.zeros(clip.shape, jnp.float32)
    for tap_row in range(3):
        for tap_col in range(3):
            spatial = spatial + flat_dot(
                padded[:, tap_row : tap_row + row_count, tap_col : tap_col + col_count],
                spatial_weight[tap_row, tap_col],
            )
    middle = spatial.astype(jnp.bfloat16)
    earlier = shifted(middle, "tm", 1)
    history = jnp.concatenate([earlier, middle], axis=0)
    temporal = jnp.zeros(clip.shape, jnp.float32)
    for time_lag in range(3):
        temporal = temporal + flat_dot(
            history[2 - time_lag : 2 - time_lag + frame_count], temporal_weight[time_lag]
        )
    output = (clip_wide + temporal).astype(jnp.bfloat16)
    later = shifted(cotangent, "tm", -1)
    future = jnp.concatenate([cotangent, later], axis=0)
    grad_wide = jnp.zeros(clip.shape, jnp.float32)
    for time_lag in range(3):
        grad_wide = grad_wide + flat_dot(
            future[time_lag : time_lag + frame_count], temporal_weight[time_lag].T
        )
    grad_mid = grad_wide.astype(jnp.bfloat16)
    grad_temporal = jnp.stack(
        [
            outer_sum(history[2 - time_lag : 2 - time_lag + frame_count], cotangent)
            for time_lag in range(3)
        ]
    )
    grad_ext = extended(grad_mid, (("height", 1),), 1)
    grad_pad = jnp.pad(grad_ext, ((0, 0), (0, 0), (1, 1), (0, 0)))
    terms = []
    for tap_row in range(3):
        for tap_col in range(3):
            terms.append(
                outer_sum(
                    padded[:, tap_row : tap_row + row_count, tap_col : tap_col + col_count],
                    grad_mid,
                )
            )
    grad_spatial = jnp.stack(terms)
    grad_act = jnp.zeros(clip.shape, jnp.float32)
    for tap_row in range(3):
        for tap_col in range(3):
            grad_act = grad_act + flat_dot(
                grad_pad[
                    :, 2 - tap_row : 2 - tap_row + row_count, 2 - tap_col : 2 - tap_col + col_count
                ],
                spatial_weight[tap_row, tap_col].T,
            )
    unused, pullback = jax.vjp(activate, clip_wide)
    grad_clip = (cotangent.astype(jnp.float32) + pullback(grad_act)[0]).astype(jnp.bfloat16)
    time_shards = lax.axis_size("tm")
    row_shards = lax.axis_size("height")
    grad_scale = 1.0 / math.sqrt(frame_count * time_shards * row_count * row_shards * col_count)
    devices = time_shards * row_shards
    spatial_rows = grad_spatial.reshape(devices, -1)
    temporal_rows = grad_temporal.reshape(devices, -1)
    packed = jnp.concatenate([spatial_rows, temporal_rows], axis=1)
    packed = packed.reshape(time_shards, row_shards, packed.shape[-1])
    packed = halving_scatter(packed, "tm")[0]
    packed = lax.all_to_all(packed, "height", 0, 0, tiled=True)
    packed = jnp.sum(packed, axis=0)
    packed = packed * grad_scale
    spatial_part = packed[: spatial_rows.shape[1]]
    temporal_part = packed[spatial_rows.shape[1] :]
    return (output, grad_clip, spatial_part, temporal_part)


def solution(mesh):
    return jax.shard_map(
        shards,
        mesh=mesh,
        in_specs=(P("tm", "height", None, None), P("tm", "height", None, None), P(), P()),
        out_specs=(
            P("tm", "height", None, None),
            P("tm", "height", None, None),
            P(("tm", "height")),
            P(("tm", "height")),
        ),
        check_vma=False,
    )
```

```python
import math

import jax
import jax.numpy as jnp
from jax import lax
from jax.sharding import PartitionSpec as P

EPSILON = 1e-06


def extended(cells, sides, width):
    for axis, dim in sides:
        count = lax.axis_size(axis)
        ends = count - 1
        head = lax.slice_in_dim(cells, 0, width, axis=dim)
        tail = lax.slice_in_dim(cells, cells.shape[dim] - width, cells.shape[dim], axis=dim)
        cells = jnp.concatenate(
            [
                lax.ppermute(tail, axis, [(i, (i + 1) % count) for i in range(ends)]),
                cells,
                lax.ppermute(head, axis, [((i + 1) % count, i) for i in range(ends)]),
            ],
            axis=dim,
        )
    return cells


def shifted(block, axis, distance):
    devices = range(lax.axis_size(axis))
    route = [(i - distance, i) for i in devices if i - distance in devices]
    return lax.ppermute(block, axis, route)


def activate(values):
    scale_inv = lax.rsqrt(jnp.mean(values * values, axis=-1, keepdims=True) + EPSILON)
    return jax.nn.silu(values * scale_inv)


def flat_dot(left, weight):
    keep_shape = left.shape[:-1]
    result = jnp.dot(left.reshape(-1, left.shape[-1]), weight, preferred_element_type=jnp.float32)
    return result.reshape(keep_shape + (weight.shape[-1],))


def outer_sum(left, right):
    channels = left.shape[-1]
    return lax.dot_general(
        left.reshape(-1, channels),
        right.reshape(-1, channels),
        (((0,), (0,)), ((), ())),
        preferred_element_type=jnp.float32,
    )


def halving_scatter(block, axis):
    count = lax.axis_size(axis)
    index = lax.axis_index(axis)
    step = 1
    while count // step % 2 == 0:
        rest = block.shape[1:]
        pairs = block.reshape((block.shape[0] // 2, 2) + rest)
        mine = index // step % 2
        keep = lax.dynamic_index_in_dim(pairs, mine, axis=1, keepdims=False)
        send = lax.dynamic_index_in_dim(pairs, 1 - mine, axis=1, keepdims=False)
        route = [(i, i ^ step) for i in range(count)]
        block = keep + lax.ppermute(send, axis, route)
        step *= 2
    ways = count // step
    if ways > 1:
        group = index // step
        total = lax.dynamic_index_in_dim(block, group, axis=0, keepdims=True)
        for shift in range(1, ways):
            route = [(i, (i + shift * step) % count) for i in range(count)]
            row = lax.dynamic_index_in_dim(block, (group + shift) % ways, axis=0, keepdims=True)
            total = total + lax.ppermute(row, axis, route)
        block = total
    return block


def shards(clip, cotangent, spatial_weight, temporal_weight):
    frame_count, row_count, col_count, channels = clip.shape
    clip_wide = clip.astype(jnp.float32)
    activated = activate(clip_wide).astype(jnp.bfloat16)
    act_ext = extended(activated, (("height", 1),), 1)
    padded = jnp.pad(act_ext, ((0, 0), (0, 0), (1, 1), (0, 0)))
    spatial = jnp.zeros(clip.shape, jnp.float32)
    for tap_row in range(3):
        for tap_col in range(3):
            spatial = spatial + flat_dot(
                padded[:, tap_row : tap_row + row_count, tap_col : tap_col + col_count],
                spatial_weight[tap_row, tap_col],
            )
    middle = spatial.astype(jnp.bfloat16)
    earlier = shifted(middle, "tm", 1)
    history = jnp.concatenate([earlier, middle], axis=0)
    temporal = jnp.zeros(clip.shape, jnp.float32)
    for time_lag in range(3):
        temporal = temporal + flat_dot(
            history[2 - time_lag : 2 - time_lag + frame_count], temporal_weight[time_lag]
        )
    output = (clip_wide + temporal).astype(jnp.bfloat16)
    later = shifted(cotangent, "tm", -1)
    future = jnp.concatenate([cotangent, later], axis=0)
    grad_wide = jnp.zeros(clip.shape, jnp.float32)
    for time_lag in range(3):
        grad_wide = grad_wide + flat_dot(
            future[time_lag : time_lag + frame_count], temporal_weight[time_lag].T
        )
    grad_mid = grad_wide.astype(jnp.bfloat16)
    grad_temporal = jnp.stack(
        [
            outer_sum(history[2 - time_lag : 2 - time_lag + frame_count], cotangent)
            for time_lag in range(3)
        ]
    )
    grad_mid_late, unused_history = lax.optimization_barrier((grad_mid, earlier))
    grad_ext = extended(grad_mid_late, (("height", 1),), 1)
    grad_pad = jnp.pad(grad_ext, ((0, 0), (0, 0), (1, 1), (0, 0)))
    terms = []
    for tap_row in range(3):
        for tap_col in range(3):
            terms.append(
                outer_sum(
                    padded[:, tap_row : tap_row + row_count, tap_col : tap_col + col_count],
                    grad_mid,
                )
            )
    grad_spatial = jnp.stack(terms)
    grad_act = jnp.zeros(clip.shape, jnp.float32)
    for tap_row in range(3):
        for tap_col in range(3):
            grad_act = grad_act + flat_dot(
                grad_pad[
                    :, 2 - tap_row : 2 - tap_row + row_count, 2 - tap_col : 2 - tap_col + col_count
                ],
                spatial_weight[tap_row, tap_col].T,
            )
    unused, pullback = jax.vjp(activate, clip_wide)
    grad_clip = (cotangent.astype(jnp.float32) + pullback(grad_act)[0]).astype(jnp.bfloat16)
    time_shards = lax.axis_size("tm")
    row_shards = lax.axis_size("height")
    grad_scale = 1.0 / math.sqrt(frame_count * time_shards * row_count * row_shards * col_count)
    devices = time_shards * row_shards
    spatial_rows = grad_spatial.reshape(devices, -1)
    temporal_rows = grad_temporal.reshape(devices, -1)
    packed = jnp.concatenate([spatial_rows, temporal_rows], axis=1)
    packed = packed.reshape(time_shards, row_shards, packed.shape[-1])
    packed = halving_scatter(packed, "tm")[0]
    packed = lax.all_to_all(packed, "height", 0, 0, tiled=True)
    packed = jnp.sum(packed, axis=0)
    packed = packed * grad_scale
    spatial_part = packed[: spatial_rows.shape[1]]
    temporal_part = packed[spatial_rows.shape[1] :]
    return (output, grad_clip, spatial_part, temporal_part)


def solution(mesh):
    return jax.shard_map(
        shards,
        mesh=mesh,
        in_specs=(P("tm", "height", None, None), P("tm", "height", None, None), P(), P()),
        out_specs=(
            P("tm", "height", None, None),
            P("tm", "height", None, None),
            P(("tm", "height")),
            P(("tm", "height")),
        ),
        check_vma=False,
    )
```

```python
import math

import jax
import jax.numpy as jnp
from jax import lax
from jax.sharding import PartitionSpec as P

EPSILON = 1e-06


def extended(cells, sides, width):
    for axis, dim in sides:
        count = lax.axis_size(axis)
        ends = count - 1
        head = lax.slice_in_dim(cells, 0, width, axis=dim)
        tail = lax.slice_in_dim(cells, cells.shape[dim] - width, cells.shape[dim], axis=dim)
        cells = jnp.concatenate(
            [
                lax.ppermute(tail, axis, [(i, (i + 1) % count) for i in range(ends)]),
                cells,
                lax.ppermute(head, axis, [((i + 1) % count, i) for i in range(ends)]),
            ],
            axis=dim,
        )
    return cells


def shifted(block, axis, distance):
    devices = range(lax.axis_size(axis))
    route = [(i - distance, i) for i in devices if i - distance in devices]
    return lax.ppermute(block, axis, route)


def activate(values):
    scale_inv = lax.rsqrt(jnp.mean(values * values, axis=-1, keepdims=True) + EPSILON)
    return jax.nn.silu(values * scale_inv)


def flat_dot(left, weight):
    keep_shape = left.shape[:-1]
    result = jnp.dot(left.reshape(-1, left.shape[-1]), weight, preferred_element_type=jnp.float32)
    return result.reshape(keep_shape + (weight.shape[-1],))


def outer_sum(left, right):
    channels = left.shape[-1]
    return lax.dot_general(
        left.reshape(-1, channels),
        right.reshape(-1, channels),
        (((0,), (0,)), ((), ())),
        preferred_element_type=jnp.float32,
    )


def halving_scatter(block, axis, tie=None, tie_after=0):
    count = lax.axis_size(axis)
    index = lax.axis_index(axis)
    step = 1
    while count // step % 2 == 0:
        rest = block.shape[1:]
        pairs = block.reshape((block.shape[0] // 2, 2) + rest)
        mine = index // step % 2
        keep = lax.dynamic_index_in_dim(pairs, mine, axis=1, keepdims=False)
        send = lax.dynamic_index_in_dim(pairs, 1 - mine, axis=1, keepdims=False)
        route = [(i, i ^ step) for i in range(count)]
        block = keep + lax.ppermute(send, axis, route)
        if tie is not None and step == 1 << tie_after:
            block, tie = lax.optimization_barrier((block, tie))
        step *= 2
    ways = count // step
    if ways > 1:
        group = index // step
        total = lax.dynamic_index_in_dim(block, group, axis=0, keepdims=True)
        for shift in range(1, ways):
            route = [(i, (i + shift * step) % count) for i in range(count)]
            row = lax.dynamic_index_in_dim(block, (group + shift) % ways, axis=0, keepdims=True)
            total = total + lax.ppermute(row, axis, route)
        block = total
    return block, tie


def shards(clip, cotangent, spatial_weight, temporal_weight):
    frame_count, row_count, col_count, channels = clip.shape
    clip_wide = clip.astype(jnp.float32)
    activated = activate(clip_wide).astype(jnp.bfloat16)
    act_ext = extended(activated, (("height", 1),), 1)
    padded = jnp.pad(act_ext, ((0, 0), (0, 0), (1, 1), (0, 0)))
    spatial = jnp.zeros(clip.shape, jnp.float32)
    for tap_row in range(3):
        for tap_col in range(3):
            spatial = spatial + flat_dot(
                padded[:, tap_row : tap_row + row_count, tap_col : tap_col + col_count],
                spatial_weight[tap_row, tap_col],
            )
    middle = spatial.astype(jnp.bfloat16)
    earlier = shifted(middle, "tm", 1)
    history = jnp.concatenate([earlier, middle], axis=0)
    temporal = jnp.zeros(clip.shape, jnp.float32)
    for time_lag in range(3):
        temporal = temporal + flat_dot(
            history[2 - time_lag : 2 - time_lag + frame_count], temporal_weight[time_lag]
        )
    output = (clip_wide + temporal).astype(jnp.bfloat16)
    later = shifted(cotangent, "tm", -1)
    future = jnp.concatenate([cotangent, later], axis=0)
    grad_wide = jnp.zeros(clip.shape, jnp.float32)
    for time_lag in range(3):
        grad_wide = grad_wide + flat_dot(
            future[time_lag : time_lag + frame_count], temporal_weight[time_lag].T
        )
    grad_mid = grad_wide.astype(jnp.bfloat16)
    grad_temporal = jnp.stack(
        [
            outer_sum(history[2 - time_lag : 2 - time_lag + frame_count], cotangent)
            for time_lag in range(3)
        ]
    )
    terms = []
    for tap_row in range(3):
        for tap_col in range(3):
            terms.append(
                outer_sum(
                    padded[:, tap_row : tap_row + row_count, tap_col : tap_col + col_count],
                    grad_mid,
                )
            )
    grad_spatial = jnp.stack(terms)
    grad_mid_late, unused_history = lax.optimization_barrier((grad_mid, earlier))
    time_shards = lax.axis_size("tm")
    row_shards = lax.axis_size("height")
    grad_scale = 1.0 / math.sqrt(frame_count * time_shards * row_count * row_shards * col_count)
    devices = time_shards * row_shards
    spatial_rows = grad_spatial.reshape(devices, -1)
    temporal_rows = grad_temporal.reshape(devices, -1)
    packed = jnp.concatenate([spatial_rows, temporal_rows], axis=1)
    packed = packed.reshape(time_shards, row_shards, packed.shape[-1])
    packed, grad_mid_late = halving_scatter(packed, "tm", grad_mid_late, 1)
    packed = packed[0]
    grad_ext = extended(grad_mid_late, (("height", 1),), 1)
    grad_pad = jnp.pad(grad_ext, ((0, 0), (0, 0), (1, 1), (0, 0)))
    grad_act = jnp.zeros(clip.shape, jnp.float32)
    for tap_row in range(3):
        for tap_col in range(3):
            grad_act = grad_act + flat_dot(
                grad_pad[
                    :, 2 - tap_row : 2 - tap_row + row_count, 2 - tap_col : 2 - tap_col + col_count
                ],
                spatial_weight[tap_row, tap_col].T,
            )
    unused, pullback = jax.vjp(activate, clip_wide)
    grad_clip = (cotangent.astype(jnp.float32) + pullback(grad_act)[0]).astype(jnp.bfloat16)
    packed = lax.all_to_all(packed, "height", 0, 0, tiled=True)
    packed = jnp.sum(packed, axis=0)
    packed = packed * grad_scale
    spatial_part = packed[: spatial_rows.shape[1]]
    temporal_part = packed[spatial_rows.shape[1] :]
    return (output, grad_clip, spatial_part, temporal_part)


def solution(mesh):
    return jax.shard_map(
        shards,
        mesh=mesh,
        in_specs=(P("tm", "height", None, None), P("tm", "height", None, None), P(), P()),
        out_specs=(
            P("tm", "height", None, None),
            P("tm", "height", None, None),
            P(("tm", "height")),
            P(("tm", "height")),
        ),
        check_vma=False,
    )
```

```python
import math

import jax
import jax.numpy as jnp
from jax import lax
from jax.sharding import PartitionSpec as P

EPSILON = 1e-06


def extended(cells, sides, width):
    for axis, dim in sides:
        count = lax.axis_size(axis)
        ends = count - 1
        head = lax.slice_in_dim(cells, 0, width, axis=dim)
        tail = lax.slice_in_dim(cells, cells.shape[dim] - width, cells.shape[dim], axis=dim)
        cells = jnp.concatenate(
            [
                lax.ppermute(tail, axis, [(i, (i + 1) % count) for i in range(ends)]),
                cells,
                lax.ppermute(head, axis, [((i + 1) % count, i) for i in range(ends)]),
            ],
            axis=dim,
        )
    return cells


def shifted(block, axis, distance):
    devices = range(lax.axis_size(axis))
    route = [(i - distance, i) for i in devices if i - distance in devices]
    return lax.ppermute(block, axis, route)


def activate(values):
    scale_inv = lax.rsqrt(jnp.mean(values * values, axis=-1, keepdims=True) + EPSILON)
    return jax.nn.silu(values * scale_inv)


def flat_dot(left, weight):
    keep_shape = left.shape[:-1]
    result = jnp.dot(left.reshape(-1, left.shape[-1]), weight, preferred_element_type=jnp.float32)
    return result.reshape(keep_shape + (weight.shape[-1],))


def outer_sum(left, right):
    channels = left.shape[-1]
    return lax.dot_general(
        left.reshape(-1, channels),
        right.reshape(-1, channels),
        (((0,), (0,)), ((), ())),
        preferred_element_type=jnp.float32,
    )


def stacked_outer_sum(lefts, right):
    channels = right.shape[-1]
    stack = jnp.stack([left.reshape(-1, channels) for left in lefts])
    return lax.dot_general(
        stack,
        right.reshape(-1, channels),
        (((1,), (0,)), ((), ())),
        preferred_element_type=jnp.float32,
    )


def halving_scatter(block, axis, tie=None, tie_after=0):
    count = lax.axis_size(axis)
    index = lax.axis_index(axis)
    step = 1
    while count // step % 2 == 0:
        rest = block.shape[1:]
        pairs = block.reshape((block.shape[0] // 2, 2) + rest)
        mine = index // step % 2
        keep = lax.dynamic_index_in_dim(pairs, mine, axis=1, keepdims=False)
        send = lax.dynamic_index_in_dim(pairs, 1 - mine, axis=1, keepdims=False)
        route = [(i, i ^ step) for i in range(count)]
        block = keep + lax.ppermute(send, axis, route)
        if tie is not None and step == 1 << tie_after:
            block, tie = lax.optimization_barrier((block, tie))
        step *= 2
    ways = count // step
    if ways > 1:
        group = index // step
        total = lax.dynamic_index_in_dim(block, group, axis=0, keepdims=True)
        for shift in range(1, ways):
            route = [(i, (i + shift * step) % count) for i in range(count)]
            row = lax.dynamic_index_in_dim(block, (group + shift) % ways, axis=0, keepdims=True)
            total = total + lax.ppermute(row, axis, route)
        block = total
    return block, tie


def shards(clip, cotangent, spatial_weight, temporal_weight):
    frame_count, row_count, col_count, channels = clip.shape
    clip_wide = clip.astype(jnp.float32)
    activated = activate(clip_wide).astype(jnp.bfloat16)
    act_ext = extended(activated, (("height", 1),), 1)
    padded = jnp.pad(act_ext, ((0, 0), (0, 0), (1, 1), (0, 0)))
    spatial = jnp.zeros(clip.shape, jnp.float32)
    for tap_row in range(3):
        for tap_col in range(3):
            spatial = spatial + flat_dot(
                padded[:, tap_row : tap_row + row_count, tap_col : tap_col + col_count],
                spatial_weight[tap_row, tap_col],
            )
    middle = spatial.astype(jnp.bfloat16)
    earlier = shifted(middle, "tm", 1)
    history = jnp.concatenate([earlier, middle], axis=0)
    temporal = jnp.zeros(clip.shape, jnp.float32)
    for time_lag in range(3):
        temporal = temporal + flat_dot(
            history[2 - time_lag : 2 - time_lag + frame_count], temporal_weight[time_lag]
        )
    output = (clip_wide + temporal).astype(jnp.bfloat16)
    later = shifted(cotangent, "tm", -1)
    future = jnp.concatenate([cotangent, later], axis=0)
    grad_wide = jnp.zeros(clip.shape, jnp.float32)
    for time_lag in range(3):
        grad_wide = grad_wide + flat_dot(
            future[time_lag : time_lag + frame_count], temporal_weight[time_lag].T
        )
    grad_mid = grad_wide.astype(jnp.bfloat16)
    grad_temporal = stacked_outer_sum(
        [history[2 - time_lag : 2 - time_lag + frame_count] for time_lag in range(3)], cotangent
    )
    grad_spatial = stacked_outer_sum(
        [
            padded[:, tap_row : tap_row + row_count, tap_col : tap_col + col_count]
            for tap_row in range(3)
            for tap_col in range(3)
        ],
        grad_mid,
    )
    grad_mid_late, unused_history = lax.optimization_barrier((grad_mid, earlier))
    time_shards = lax.axis_size("tm")
    row_shards = lax.axis_size("height")
    grad_scale = 1.0 / math.sqrt(frame_count * time_shards * row_count * row_shards * col_count)
    devices = time_shards * row_shards
    spatial_rows = grad_spatial.reshape(devices, -1)
    temporal_rows = grad_temporal.reshape(devices, -1)
    packed = jnp.concatenate([spatial_rows, temporal_rows], axis=1)
    packed = packed.reshape(time_shards, row_shards, packed.shape[-1])
    packed, grad_mid_late = halving_scatter(packed, "tm", grad_mid_late, 1)
    packed = packed[0]
    grad_ext = extended(grad_mid_late, (("height", 1),), 1)
    grad_pad = jnp.pad(grad_ext, ((0, 0), (0, 0), (1, 1), (0, 0)))
    grad_act = jnp.zeros(clip.shape, jnp.float32)
    for tap_row in range(3):
        for tap_col in range(3):
            grad_act = grad_act + flat_dot(
                grad_pad[
                    :, 2 - tap_row : 2 - tap_row + row_count, 2 - tap_col : 2 - tap_col + col_count
                ],
                spatial_weight[tap_row, tap_col].T,
            )
    unused, pullback = jax.vjp(activate, clip_wide)
    grad_clip = (cotangent.astype(jnp.float32) + pullback(grad_act)[0]).astype(jnp.bfloat16)
    packed = lax.all_to_all(packed, "height", 0, 0, tiled=True)
    packed = jnp.sum(packed, axis=0)
    packed = packed * grad_scale
    spatial_part = packed[: spatial_rows.shape[1]]
    temporal_part = packed[spatial_rows.shape[1] :]
    return (output, grad_clip, spatial_part, temporal_part)


def solution(mesh):
    return jax.shard_map(
        shards,
        mesh=mesh,
        in_specs=(P("tm", "height", None, None), P("tm", "height", None, None), P(), P()),
        out_specs=(
            P("tm", "height", None, None),
            P("tm", "height", None, None),
            P(("tm", "height")),
            P(("tm", "height")),
        ),
        check_vma=False,
    )
```

```python
import math

import jax
import jax.numpy as jnp
from jax import lax
from jax.sharding import PartitionSpec as P

EPSILON = 1e-06


def extended(cells, sides, width):
    for axis, dim in sides:
        count = lax.axis_size(axis)
        ends = count - 1
        head = lax.slice_in_dim(cells, 0, width, axis=dim)
        tail = lax.slice_in_dim(cells, cells.shape[dim] - width, cells.shape[dim], axis=dim)
        cells = jnp.concatenate(
            [
                lax.ppermute(tail, axis, [(i, (i + 1) % count) for i in range(ends)]),
                cells,
                lax.ppermute(head, axis, [((i + 1) % count, i) for i in range(ends)]),
            ],
            axis=dim,
        )
    return cells


def shifted(block, axis, distance):
    devices = range(lax.axis_size(axis))
    route = [(i - distance, i) for i in devices if i - distance in devices]
    return lax.ppermute(block, axis, route)


def activate(values):
    scale_inv = lax.rsqrt(jnp.mean(values * values, axis=-1, keepdims=True) + EPSILON)
    return jax.nn.silu(values * scale_inv)


def flat_dot(left, weight):
    keep_shape = left.shape[:-1]
    result = jnp.dot(left.reshape(-1, left.shape[-1]), weight, preferred_element_type=jnp.float32)
    return result.reshape(keep_shape + (weight.shape[-1],))


def outer_sum(left, right):
    channels = left.shape[-1]
    return lax.dot_general(
        left.reshape(-1, channels),
        right.reshape(-1, channels),
        (((0,), (0,)), ((), ())),
        preferred_element_type=jnp.float32,
    )


def halving_scatter(block, axis, tie=None, tie_after=0, narrow_from=None):
    count = lax.axis_size(axis)
    index = lax.axis_index(axis)
    step = 1
    while count // step % 2 == 0:
        rest = block.shape[1:]
        pairs = block.reshape((block.shape[0] // 2, 2) + rest)
        mine = index // step % 2
        keep = lax.dynamic_index_in_dim(pairs, mine, axis=1, keepdims=False)
        send = lax.dynamic_index_in_dim(pairs, 1 - mine, axis=1, keepdims=False)
        route = [(i, i ^ step) for i in range(count)]
        if narrow_from is not None and step >= narrow_from:
            sent = lax.ppermute(send.astype(jnp.bfloat16), axis, route).astype(block.dtype)
        else:
            sent = lax.ppermute(send, axis, route)
        block = keep + sent
        if tie is not None and step == 1 << tie_after:
            block, tie = lax.optimization_barrier((block, tie))
        step *= 2
    ways = count // step
    if ways > 1:
        group = index // step
        total = lax.dynamic_index_in_dim(block, group, axis=0, keepdims=True)
        for shift in range(1, ways):
            route = [(i, (i + shift * step) % count) for i in range(count)]
            row = lax.dynamic_index_in_dim(block, (group + shift) % ways, axis=0, keepdims=True)
            total = total + lax.ppermute(row, axis, route)
        block = total
    return block, tie


def shards(clip, cotangent, spatial_weight, temporal_weight):
    frame_count, row_count, col_count, channels = clip.shape
    clip_wide = clip.astype(jnp.float32)
    activated = activate(clip_wide).astype(jnp.bfloat16)
    act_ext = extended(activated, (("height", 1),), 1)
    padded = jnp.pad(act_ext, ((0, 0), (0, 0), (1, 1), (0, 0)))
    spatial = jnp.zeros(clip.shape, jnp.float32)
    for tap_row in range(3):
        for tap_col in range(3):
            spatial = spatial + flat_dot(
                padded[:, tap_row : tap_row + row_count, tap_col : tap_col + col_count],
                spatial_weight[tap_row, tap_col],
            )
    middle = spatial.astype(jnp.bfloat16)
    earlier = shifted(middle, "tm", 1)
    history = jnp.concatenate([earlier, middle], axis=0)
    temporal = jnp.zeros(clip.shape, jnp.float32)
    for time_lag in range(3):
        temporal = temporal + flat_dot(
            history[2 - time_lag : 2 - time_lag + frame_count], temporal_weight[time_lag]
        )
    output = (clip_wide + temporal).astype(jnp.bfloat16)
    later = shifted(cotangent, "tm", -1)
    future = jnp.concatenate([cotangent, later], axis=0)
    grad_wide = jnp.zeros(clip.shape, jnp.float32)
    for time_lag in range(3):
        grad_wide = grad_wide + flat_dot(
            future[time_lag : time_lag + frame_count], temporal_weight[time_lag].T
        )
    grad_mid = grad_wide.astype(jnp.bfloat16)
    grad_temporal = jnp.stack(
        [
            outer_sum(history[2 - time_lag : 2 - time_lag + frame_count], cotangent)
            for time_lag in range(3)
        ]
    )
    terms = []
    for tap_row in range(3):
        for tap_col in range(3):
            terms.append(
                outer_sum(
                    padded[:, tap_row : tap_row + row_count, tap_col : tap_col + col_count],
                    grad_mid,
                )
            )
    grad_spatial = jnp.stack(terms)
    grad_mid_late, unused_history = lax.optimization_barrier((grad_mid, earlier))
    time_shards = lax.axis_size("tm")
    row_shards = lax.axis_size("height")
    grad_scale = 1.0 / math.sqrt(frame_count * time_shards * row_count * row_shards * col_count)
    devices = time_shards * row_shards
    spatial_rows = grad_spatial.reshape(devices, -1)
    temporal_rows = grad_temporal.reshape(devices, -1)
    packed = jnp.concatenate([spatial_rows, temporal_rows], axis=1)
    packed = packed.reshape(time_shards, row_shards, packed.shape[-1])
    packed, grad_mid_late = halving_scatter(packed, "tm", grad_mid_late, 1, narrow_from=2)
    packed = packed[0]
    grad_ext = extended(grad_mid_late, (("height", 1),), 1)
    grad_pad = jnp.pad(grad_ext, ((0, 0), (0, 0), (1, 1), (0, 0)))
    grad_act = jnp.zeros(clip.shape, jnp.float32)
    for tap_row in range(3):
        for tap_col in range(3):
            grad_act = grad_act + flat_dot(
                grad_pad[
                    :, 2 - tap_row : 2 - tap_row + row_count, 2 - tap_col : 2 - tap_col + col_count
                ],
                spatial_weight[tap_row, tap_col].T,
            )
    unused, pullback = jax.vjp(activate, clip_wide)
    grad_clip = (cotangent.astype(jnp.float32) + pullback(grad_act)[0]).astype(jnp.bfloat16)
    packed = lax.all_to_all(packed, "height", 0, 0, tiled=True)
    packed = jnp.sum(packed, axis=0)
    packed = packed * grad_scale
    spatial_part = packed[: spatial_rows.shape[1]]
    temporal_part = packed[spatial_rows.shape[1] :]
    return (output, grad_clip, spatial_part, temporal_part)


def solution(mesh):
    return jax.shard_map(
        shards,
        mesh=mesh,
        in_specs=(P("tm", "height", None, None), P("tm", "height", None, None), P(), P()),
        out_specs=(
            P("tm", "height", None, None),
            P("tm", "height", None, None),
            P(("tm", "height")),
            P(("tm", "height")),
        ),
        check_vma=False,
    )
```

```python
import math

import jax
import jax.numpy as jnp
from jax import lax
from jax.sharding import PartitionSpec as P

EPSILON = 1e-06


def extended(cells, sides, width):
    for axis, dim in sides:
        count = lax.axis_size(axis)
        ends = count - 1
        head = lax.slice_in_dim(cells, 0, width, axis=dim)
        tail = lax.slice_in_dim(cells, cells.shape[dim] - width, cells.shape[dim], axis=dim)
        cells = jnp.concatenate(
            [
                lax.ppermute(tail, axis, [(i, (i + 1) % count) for i in range(ends)]),
                cells,
                lax.ppermute(head, axis, [((i + 1) % count, i) for i in range(ends)]),
            ],
            axis=dim,
        )
    return cells


def shifted(block, axis, distance):
    devices = range(lax.axis_size(axis))
    route = [(i - distance, i) for i in devices if i - distance in devices]
    return lax.ppermute(block, axis, route)


def activate(values):
    scale_inv = lax.rsqrt(jnp.mean(values * values, axis=-1, keepdims=True) + EPSILON)
    return jax.nn.silu(values * scale_inv)


def flat_dot(left, weight):
    keep_shape = left.shape[:-1]
    result = jnp.dot(left.reshape(-1, left.shape[-1]), weight, preferred_element_type=jnp.float32)
    return result.reshape(keep_shape + (weight.shape[-1],))


def outer_sum(left, right):
    channels = left.shape[-1]
    return lax.dot_general(
        left.reshape(-1, channels),
        right.reshape(-1, channels),
        (((0,), (0,)), ((), ())),
        preferred_element_type=jnp.float32,
    )


def halving_scatter(block, axis, tie=None, tie_after=0, narrow_from=None):
    count = lax.axis_size(axis)
    index = lax.axis_index(axis)
    step = 1
    while count // step % 2 == 0:
        rest = block.shape[1:]
        pairs = block.reshape((block.shape[0] // 2, 2) + rest)
        mine = index // step % 2
        keep = lax.dynamic_index_in_dim(pairs, mine, axis=1, keepdims=False)
        send = lax.dynamic_index_in_dim(pairs, 1 - mine, axis=1, keepdims=False)
        route = [(i, i ^ step) for i in range(count)]
        if narrow_from is not None and step >= narrow_from:
            sent = lax.ppermute(send.astype(jnp.bfloat16), axis, route).astype(block.dtype)
        else:
            sent = lax.ppermute(send, axis, route)
        block = keep + sent
        if tie is not None and step == 1 << tie_after:
            block, tie = lax.optimization_barrier((block, tie))
        step *= 2
    ways = count // step
    if ways > 1:
        group = index // step
        total = lax.dynamic_index_in_dim(block, group, axis=0, keepdims=True)
        for shift in range(1, ways):
            route = [(i, (i + shift * step) % count) for i in range(count)]
            row = lax.dynamic_index_in_dim(block, (group + shift) % ways, axis=0, keepdims=True)
            total = total + lax.ppermute(row, axis, route)
        block = total
    return block, tie


def shards(clip, cotangent, spatial_weight, temporal_weight):
    frame_count, row_count, col_count, channels = clip.shape
    clip_wide = clip.astype(jnp.float32)
    activated = activate(clip_wide).astype(jnp.bfloat16)
    act_ext = extended(activated, (("height", 1),), 1)
    padded = jnp.pad(act_ext, ((0, 0), (0, 0), (1, 1), (0, 0)))
    spatial = jnp.zeros(clip.shape, jnp.float32)
    for tap_row in range(3):
        for tap_col in range(3):
            spatial = spatial + flat_dot(
                padded[:, tap_row : tap_row + row_count, tap_col : tap_col + col_count],
                spatial_weight[tap_row, tap_col],
            )
    middle = spatial.astype(jnp.bfloat16)
    earlier = shifted(middle, "tm", 1)
    history = jnp.concatenate([earlier, middle], axis=0)
    temporal = jnp.zeros(clip.shape, jnp.float32)
    for time_lag in range(3):
        temporal = temporal + flat_dot(
            history[2 - time_lag : 2 - time_lag + frame_count], temporal_weight[time_lag]
        )
    output = (clip_wide + temporal).astype(jnp.bfloat16)
    later = shifted(cotangent, "tm", -1)
    future = jnp.concatenate([cotangent, later], axis=0)
    grad_wide = jnp.zeros(clip.shape, jnp.float32)
    for time_lag in range(3):
        grad_wide = grad_wide + flat_dot(
            future[time_lag : time_lag + frame_count], temporal_weight[time_lag].T
        )
    grad_mid = grad_wide.astype(jnp.bfloat16)
    grad_temporal = jnp.stack(
        [
            outer_sum(history[2 - time_lag : 2 - time_lag + frame_count], cotangent)
            for time_lag in range(3)
        ]
    )
    terms = []
    for tap_row in range(3):
        for tap_col in range(3):
            terms.append(
                outer_sum(
                    padded[:, tap_row : tap_row + row_count, tap_col : tap_col + col_count],
                    grad_mid,
                )
            )
    grad_spatial = jnp.stack(terms)
    grad_mid_late, unused_history = lax.optimization_barrier((grad_mid, earlier))
    time_shards = lax.axis_size("tm")
    row_shards = lax.axis_size("height")
    grad_scale = 1.0 / math.sqrt(frame_count * time_shards * row_count * row_shards * col_count)
    devices = time_shards * row_shards
    spatial_rows = grad_spatial.reshape(devices, -1)
    temporal_rows = grad_temporal.reshape(devices, -1)
    packed = jnp.concatenate([spatial_rows, temporal_rows], axis=1)
    packed = packed.reshape(time_shards, row_shards, packed.shape[-1])
    packed, grad_mid_late = halving_scatter(packed, "tm", grad_mid_late, 2, narrow_from=2)
    packed = packed[0]
    grad_ext = extended(grad_mid_late, (("height", 1),), 1)
    grad_pad = jnp.pad(grad_ext, ((0, 0), (0, 0), (1, 1), (0, 0)))
    grad_act = jnp.zeros(clip.shape, jnp.float32)
    for tap_row in range(3):
        for tap_col in range(3):
            grad_act = grad_act + flat_dot(
                grad_pad[
                    :, 2 - tap_row : 2 - tap_row + row_count, 2 - tap_col : 2 - tap_col + col_count
                ],
                spatial_weight[tap_row, tap_col].T,
            )
    unused, pullback = jax.vjp(activate, clip_wide)
    grad_clip = (cotangent.astype(jnp.float32) + pullback(grad_act)[0]).astype(jnp.bfloat16)
    packed = lax.all_to_all(packed, "height", 0, 0, tiled=True)
    packed = jnp.sum(packed, axis=0)
    packed = packed * grad_scale
    spatial_part = packed[: spatial_rows.shape[1]]
    temporal_part = packed[spatial_rows.shape[1] :]
    return (output, grad_clip, spatial_part, temporal_part)


def solution(mesh):
    return jax.shard_map(
        shards,
        mesh=mesh,
        in_specs=(P("tm", "height", None, None), P("tm", "height", None, None), P(), P()),
        out_specs=(
            P("tm", "height", None, None),
            P("tm", "height", None, None),
            P(("tm", "height")),
            P(("tm", "height")),
        ),
        check_vma=False,
    )
```

```python
import math

import jax
import jax.numpy as jnp
from jax import lax
from jax.sharding import PartitionSpec as P

EPSILON = 1e-06


def extended(cells, sides, width):
    for axis, dim in sides:
        count = lax.axis_size(axis)
        ends = count - 1
        head = lax.slice_in_dim(cells, 0, width, axis=dim)
        tail = lax.slice_in_dim(cells, cells.shape[dim] - width, cells.shape[dim], axis=dim)
        cells = jnp.concatenate(
            [
                lax.ppermute(tail, axis, [(i, (i + 1) % count) for i in range(ends)]),
                cells,
                lax.ppermute(head, axis, [((i + 1) % count, i) for i in range(ends)]),
            ],
            axis=dim,
        )
    return cells


def shifted(block, axis, distance):
    devices = range(lax.axis_size(axis))
    route = [(i - distance, i) for i in devices if i - distance in devices]
    return lax.ppermute(block, axis, route)


def activate(values):
    scale_inv = lax.rsqrt(jnp.mean(values * values, axis=-1, keepdims=True) + EPSILON)
    return jax.nn.silu(values * scale_inv)


def flat_dot(left, weight):
    keep_shape = left.shape[:-1]
    result = jnp.dot(left.reshape(-1, left.shape[-1]), weight, preferred_element_type=jnp.float32)
    return result.reshape(keep_shape + (weight.shape[-1],))


def outer_sum(left, right):
    channels = left.shape[-1]
    return lax.dot_general(
        left.reshape(-1, channels),
        right.reshape(-1, channels),
        (((0,), (0,)), ((), ())),
        preferred_element_type=jnp.float32,
    )


def halving_scatter(block, axis, tie=None, tie_after=0, narrow_from=None):
    count = lax.axis_size(axis)
    index = lax.axis_index(axis)
    step = 1
    while count // step % 2 == 0:
        rest = block.shape[1:]
        pairs = block.reshape((block.shape[0] // 2, 2) + rest)
        mine = index // step % 2
        keep = lax.dynamic_index_in_dim(pairs, mine, axis=1, keepdims=False)
        send = lax.dynamic_index_in_dim(pairs, 1 - mine, axis=1, keepdims=False)
        route = [(i, i ^ step) for i in range(count)]
        if narrow_from is not None and step >= narrow_from:
            sent = lax.ppermute(send.astype(jnp.bfloat16), axis, route).astype(block.dtype)
        else:
            sent = lax.ppermute(send, axis, route)
        block = keep + sent
        if tie is not None and step == 1 << tie_after:
            block, tie = lax.optimization_barrier((block, tie))
        step *= 2
    ways = count // step
    if ways > 1:
        group = index // step
        total = lax.dynamic_index_in_dim(block, group, axis=0, keepdims=True)
        for shift in range(1, ways):
            route = [(i, (i + shift * step) % count) for i in range(count)]
            row = lax.dynamic_index_in_dim(block, (group + shift) % ways, axis=0, keepdims=True)
            total = total + lax.ppermute(row, axis, route)
        block = total
    return block, tie


def shards(clip, cotangent, spatial_weight, temporal_weight):
    frame_count, row_count, col_count, channels = clip.shape
    clip_wide = clip.astype(jnp.float32)
    activated = activate(clip_wide).astype(jnp.bfloat16)
    act_ext = extended(activated, (("height", 1),), 1)
    padded = jnp.pad(act_ext, ((0, 0), (0, 0), (1, 1), (0, 0)))
    spatial = jnp.zeros(clip.shape, jnp.float32)
    for tap_row in range(3):
        for tap_col in range(3):
            spatial = spatial + flat_dot(
                padded[:, tap_row : tap_row + row_count, tap_col : tap_col + col_count],
                spatial_weight[tap_row, tap_col],
            )
    middle = spatial.astype(jnp.bfloat16)
    earlier = shifted(middle, "tm", 1)
    history = jnp.concatenate([earlier, middle], axis=0)
    temporal = jnp.zeros(clip.shape, jnp.float32)
    for time_lag in range(3):
        temporal = temporal + flat_dot(
            history[2 - time_lag : 2 - time_lag + frame_count], temporal_weight[time_lag]
        )
    output = (clip_wide + temporal).astype(jnp.bfloat16)
    later = shifted(cotangent, "tm", -1)
    future = jnp.concatenate([cotangent, later], axis=0)
    grad_wide = jnp.zeros(clip.shape, jnp.float32)
    for time_lag in range(3):
        grad_wide = grad_wide + flat_dot(
            future[time_lag : time_lag + frame_count], temporal_weight[time_lag].T
        )
    grad_mid = grad_wide.astype(jnp.bfloat16)
    grad_temporal = jnp.stack(
        [
            outer_sum(history[2 - time_lag : 2 - time_lag + frame_count], cotangent)
            for time_lag in range(3)
        ]
    )
    terms = []
    for tap_row in range(3):
        for tap_col in range(3):
            terms.append(
                outer_sum(
                    padded[:, tap_row : tap_row + row_count, tap_col : tap_col + col_count],
                    grad_mid,
                )
            )
    grad_spatial = jnp.stack(terms)
    grad_mid_late, unused_history = lax.optimization_barrier((grad_mid, earlier))
    time_shards = lax.axis_size("tm")
    row_shards = lax.axis_size("height")
    grad_scale = 1.0 / math.sqrt(frame_count * time_shards * row_count * row_shards * col_count)
    devices = time_shards * row_shards
    spatial_rows = grad_spatial.reshape(devices, -1)
    temporal_rows = grad_temporal.reshape(devices, -1)
    packed = jnp.concatenate([spatial_rows, temporal_rows], axis=1)
    packed = packed.reshape(time_shards, row_shards, packed.shape[-1])
    packed, grad_mid_late = halving_scatter(packed, "tm", grad_mid_late, 2, narrow_from=2)
    packed = packed[0]
    grad_ext = extended(grad_mid_late, (("height", 1),), 1)
    grad_pad = jnp.pad(grad_ext, ((0, 0), (0, 0), (1, 1), (0, 0)))
    grad_act = jnp.zeros(clip.shape, jnp.float32)
    for tap_row in range(3):
        for tap_col in range(3):
            grad_act = grad_act + flat_dot(
                grad_pad[
                    :, 2 - tap_row : 2 - tap_row + row_count, 2 - tap_col : 2 - tap_col + col_count
                ],
                spatial_weight[tap_row, tap_col].T,
            )
    unused, pullback = jax.vjp(activate, clip_wide)
    grad_clip = (cotangent.astype(jnp.float32) + pullback(grad_act)[0]).astype(jnp.bfloat16)
    packed = lax.all_to_all(packed.astype(jnp.bfloat16), "height", 0, 0, tiled=True)
    packed = jnp.sum(packed.astype(jnp.float32), axis=0)
    packed = packed * grad_scale
    spatial_part = packed[: spatial_rows.shape[1]]
    temporal_part = packed[spatial_rows.shape[1] :]
    return (output, grad_clip, spatial_part, temporal_part)


def solution(mesh):
    return jax.shard_map(
        shards,
        mesh=mesh,
        in_specs=(P("tm", "height", None, None), P("tm", "height", None, None), P(), P()),
        out_specs=(
            P("tm", "height", None, None),
            P("tm", "height", None, None),
            P(("tm", "height")),
            P(("tm", "height")),
        ),
        check_vma=False,
    )
```

```python
import math

import jax
import jax.numpy as jnp
from jax import lax
from jax.sharding import PartitionSpec as P

EPSILON = 1e-06


def extended(cells, sides, width):
    for axis, dim in sides:
        count = lax.axis_size(axis)
        ends = count - 1
        head = lax.slice_in_dim(cells, 0, width, axis=dim)
        tail = lax.slice_in_dim(cells, cells.shape[dim] - width, cells.shape[dim], axis=dim)
        cells = jnp.concatenate(
            [
                lax.ppermute(tail, axis, [(i, (i + 1) % count) for i in range(ends)]),
                cells,
                lax.ppermute(head, axis, [((i + 1) % count, i) for i in range(ends)]),
            ],
            axis=dim,
        )
    return cells


def shifted(block, axis, distance):
    devices = range(lax.axis_size(axis))
    route = [(i - distance, i) for i in devices if i - distance in devices]
    return lax.ppermute(block, axis, route)


def activate(values):
    scale_inv = lax.rsqrt(jnp.mean(values * values, axis=-1, keepdims=True) + EPSILON)
    return jax.nn.silu(values * scale_inv)


def flat_dot(left, weight):
    keep_shape = left.shape[:-1]
    result = jnp.dot(left.reshape(-1, left.shape[-1]), weight, preferred_element_type=jnp.float32)
    return result.reshape(keep_shape + (weight.shape[-1],))


def outer_sum(left, right):
    channels = left.shape[-1]
    return lax.dot_general(
        left.reshape(-1, channels),
        right.reshape(-1, channels),
        (((0,), (0,)), ((), ())),
        preferred_element_type=jnp.float32,
    )


def halving_scatter(block, axis, tie=None, tie_after=0, narrow_from=None):
    count = lax.axis_size(axis)
    index = lax.axis_index(axis)
    step = 1
    while count // step % 2 == 0:
        rest = block.shape[1:]
        pairs = block.reshape((block.shape[0] // 2, 2) + rest)
        mine = index // step % 2
        keep = lax.dynamic_index_in_dim(pairs, mine, axis=1, keepdims=False)
        send = lax.dynamic_index_in_dim(pairs, 1 - mine, axis=1, keepdims=False)
        route = [(i, i ^ step) for i in range(count)]
        if narrow_from is not None and step >= narrow_from:
            sent = lax.ppermute(send.astype(jnp.bfloat16), axis, route).astype(block.dtype)
        else:
            sent = lax.ppermute(send, axis, route)
        block = keep + sent
        if tie is not None and step == 1 << tie_after:
            block, tie = lax.optimization_barrier((block, tie))
        step *= 2
    ways = count // step
    if ways > 1:
        group = index // step
        total = lax.dynamic_index_in_dim(block, group, axis=0, keepdims=True)
        for shift in range(1, ways):
            route = [(i, (i + shift * step) % count) for i in range(count)]
            row = lax.dynamic_index_in_dim(block, (group + shift) % ways, axis=0, keepdims=True)
            total = total + lax.ppermute(row, axis, route)
        block = total
    return block, tie


def shards(clip, cotangent, spatial_weight, temporal_weight):
    frame_count, row_count, col_count, channels = clip.shape
    clip_wide = clip.astype(jnp.float32)
    activated = activate(clip_wide).astype(jnp.bfloat16)
    act_ext = extended(activated, (("height", 1),), 1)
    padded = jnp.pad(act_ext, ((0, 0), (0, 0), (1, 1), (0, 0)))
    spatial = jnp.zeros(clip.shape, jnp.float32)
    for tap_row in range(3):
        for tap_col in range(3):
            spatial = spatial + flat_dot(
                padded[:, tap_row : tap_row + row_count, tap_col : tap_col + col_count],
                spatial_weight[tap_row, tap_col],
            )
    middle = spatial.astype(jnp.bfloat16)
    earlier = shifted(middle, "tm", 1)
    history = jnp.concatenate([earlier, middle], axis=0)
    temporal = jnp.zeros(clip.shape, jnp.float32)
    for time_lag in range(3):
        temporal = temporal + flat_dot(
            history[2 - time_lag : 2 - time_lag + frame_count], temporal_weight[time_lag]
        )
    output = (clip_wide + temporal).astype(jnp.bfloat16)
    later = shifted(cotangent, "tm", -1)
    future = jnp.concatenate([cotangent, later], axis=0)
    grad_wide = jnp.zeros(clip.shape, jnp.float32)
    for time_lag in range(3):
        grad_wide = grad_wide + flat_dot(
            future[time_lag : time_lag + frame_count], temporal_weight[time_lag].T
        )
    grad_mid = grad_wide.astype(jnp.bfloat16)
    grad_temporal = jnp.stack(
        [
            outer_sum(history[2 - time_lag : 2 - time_lag + frame_count], cotangent)
            for time_lag in range(3)
        ]
    )
    grad_spatial = lax.conv_general_dilated(
        padded,
        grad_mid,
        window_strides=(1, 1),
        padding="VALID",
        dimension_numbers=("CHWN", "IHWO", "HWNC"),
        preferred_element_type=jnp.float32,
    ).reshape(9, channels, channels)
    grad_mid_late, unused_history = lax.optimization_barrier((grad_mid, earlier))
    time_shards = lax.axis_size("tm")
    row_shards = lax.axis_size("height")
    grad_scale = 1.0 / math.sqrt(frame_count * time_shards * row_count * row_shards * col_count)
    devices = time_shards * row_shards
    spatial_rows = grad_spatial.reshape(devices, -1)
    temporal_rows = grad_temporal.reshape(devices, -1)
    packed = jnp.concatenate([spatial_rows, temporal_rows], axis=1)
    packed = packed.reshape(time_shards, row_shards, packed.shape[-1])
    packed, grad_mid_late = halving_scatter(packed, "tm", grad_mid_late, 2, narrow_from=2)
    packed = packed[0]
    grad_ext = extended(grad_mid_late, (("height", 1),), 1)
    grad_pad = jnp.pad(grad_ext, ((0, 0), (0, 0), (1, 1), (0, 0)))
    grad_act = jnp.zeros(clip.shape, jnp.float32)
    for tap_row in range(3):
        for tap_col in range(3):
            grad_act = grad_act + flat_dot(
                grad_pad[
                    :, 2 - tap_row : 2 - tap_row + row_count, 2 - tap_col : 2 - tap_col + col_count
                ],
                spatial_weight[tap_row, tap_col].T,
            )
    unused, pullback = jax.vjp(activate, clip_wide)
    grad_clip = (cotangent.astype(jnp.float32) + pullback(grad_act)[0]).astype(jnp.bfloat16)
    packed = lax.all_to_all(packed, "height", 0, 0, tiled=True)
    packed = jnp.sum(packed, axis=0)
    packed = packed * grad_scale
    spatial_part = packed[: spatial_rows.shape[1]]
    temporal_part = packed[spatial_rows.shape[1] :]
    return (output, grad_clip, spatial_part, temporal_part)


def solution(mesh):
    return jax.shard_map(
        shards,
        mesh=mesh,
        in_specs=(P("tm", "height", None, None), P("tm", "height", None, None), P(), P()),
        out_specs=(
            P("tm", "height", None, None),
            P("tm", "height", None, None),
            P(("tm", "height")),
            P(("tm", "height")),
        ),
        check_vma=False,
    )
```

```python
import math

import jax
import jax.numpy as jnp
from jax import lax
from jax.sharding import PartitionSpec as P

EPSILON = 1e-06


def extended(cells, sides, width):
    for axis, dim in sides:
        count = lax.axis_size(axis)
        ends = count - 1
        head = lax.slice_in_dim(cells, 0, width, axis=dim)
        tail = lax.slice_in_dim(cells, cells.shape[dim] - width, cells.shape[dim], axis=dim)
        cells = jnp.concatenate(
            [
                lax.ppermute(tail, axis, [(i, (i + 1) % count) for i in range(ends)]),
                cells,
                lax.ppermute(head, axis, [((i + 1) % count, i) for i in range(ends)]),
            ],
            axis=dim,
        )
    return cells


def shifted(block, axis, distance):
    devices = range(lax.axis_size(axis))
    route = [(i - distance, i) for i in devices if i - distance in devices]
    return lax.ppermute(block, axis, route)


def activate(values):
    scale_inv = lax.rsqrt(jnp.mean(values * values, axis=-1, keepdims=True) + EPSILON)
    return jax.nn.silu(values * scale_inv)


def flat_dot(left, weight):
    keep_shape = left.shape[:-1]
    result = jnp.dot(left.reshape(-1, left.shape[-1]), weight, preferred_element_type=jnp.float32)
    return result.reshape(keep_shape + (weight.shape[-1],))


def outer_sum(left, right):
    channels = left.shape[-1]
    return lax.dot_general(
        left.reshape(-1, channels),
        right.reshape(-1, channels),
        (((0,), (0,)), ((), ())),
        preferred_element_type=jnp.float32,
    )


def halving_scatter(block, axis, tie=None, tie_after=0, narrow_from=None):
    count = lax.axis_size(axis)
    index = lax.axis_index(axis)
    step = 1
    while count // step % 2 == 0:
        rest = block.shape[1:]
        pairs = block.reshape((block.shape[0] // 2, 2) + rest)
        mine = index // step % 2
        keep = lax.dynamic_index_in_dim(pairs, mine, axis=1, keepdims=False)
        send = lax.dynamic_index_in_dim(pairs, 1 - mine, axis=1, keepdims=False)
        route = [(i, i ^ step) for i in range(count)]
        if narrow_from is not None and step >= narrow_from:
            sent = lax.ppermute(send.astype(jnp.bfloat16), axis, route).astype(block.dtype)
        else:
            sent = lax.ppermute(send, axis, route)
        block = keep + sent
        if tie is not None and step == 1 << tie_after:
            block, tie = lax.optimization_barrier((block, tie))
        step *= 2
    ways = count // step
    if ways > 1:
        group = index // step
        total = lax.dynamic_index_in_dim(block, group, axis=0, keepdims=True)
        for shift in range(1, ways):
            route = [(i, (i + shift * step) % count) for i in range(count)]
            row = lax.dynamic_index_in_dim(block, (group + shift) % ways, axis=0, keepdims=True)
            total = total + lax.ppermute(row, axis, route)
        block = total
    return block, tie


def shards(clip, cotangent, spatial_weight, temporal_weight):
    frame_count, row_count, col_count, channels = clip.shape
    clip_wide = clip.astype(jnp.float32)
    activated = activate(clip_wide).astype(jnp.bfloat16)
    act_ext = extended(activated, (("height", 1),), 1)
    padded = jnp.pad(act_ext, ((0, 0), (0, 0), (1, 1), (0, 0)))
    spatial = lax.conv_general_dilated(
        padded,
        spatial_weight,
        window_strides=(1, 1),
        padding="VALID",
        dimension_numbers=("NHWC", "HWIO", "NHWC"),
        preferred_element_type=jnp.float32,
    )
    middle = spatial.astype(jnp.bfloat16)
    earlier = shifted(middle, "tm", 1)
    history = jnp.concatenate([earlier, middle], axis=0)
    temporal = jnp.zeros(clip.shape, jnp.float32)
    for time_lag in range(3):
        temporal = temporal + flat_dot(
            history[2 - time_lag : 2 - time_lag + frame_count], temporal_weight[time_lag]
        )
    output = (clip_wide + temporal).astype(jnp.bfloat16)
    later = shifted(cotangent, "tm", -1)
    future = jnp.concatenate([cotangent, later], axis=0)
    grad_wide = jnp.zeros(clip.shape, jnp.float32)
    for time_lag in range(3):
        grad_wide = grad_wide + flat_dot(
            future[time_lag : time_lag + frame_count], temporal_weight[time_lag].T
        )
    grad_mid = grad_wide.astype(jnp.bfloat16)
    grad_temporal = lax.conv_general_dilated(
        history.reshape(history.shape[0], -1, channels),
        cotangent.reshape(frame_count, -1, channels),
        window_strides=(1,),
        padding="VALID",
        dimension_numbers=("WCN", "WIO", "WNC"),
        preferred_element_type=jnp.float32,
    )[::-1]
    grad_spatial = lax.conv_general_dilated(
        padded,
        grad_mid,
        window_strides=(1, 1),
        padding="VALID",
        dimension_numbers=("CHWN", "IHWO", "HWNC"),
        preferred_element_type=jnp.float32,
    ).reshape(9, channels, channels)
    grad_mid_late, unused_history = lax.optimization_barrier((grad_mid, earlier))
    time_shards = lax.axis_size("tm")
    row_shards = lax.axis_size("height")
    grad_scale = 1.0 / math.sqrt(frame_count * time_shards * row_count * row_shards * col_count)
    devices = time_shards * row_shards
    spatial_rows = grad_spatial.reshape(devices, -1)
    temporal_rows = grad_temporal.reshape(devices, -1)
    packed = jnp.concatenate([spatial_rows, temporal_rows], axis=1)
    packed = packed.reshape(time_shards, row_shards, packed.shape[-1])
    packed, grad_mid_late = halving_scatter(packed, "tm", grad_mid_late, 2, narrow_from=2)
    packed = packed[0]
    grad_ext = extended(grad_mid_late, (("height", 1),), 1)
    grad_pad = jnp.pad(grad_ext, ((0, 0), (0, 0), (1, 1), (0, 0)))
    grad_act = jnp.zeros(clip.shape, jnp.float32)
    for tap_row in range(3):
        for tap_col in range(3):
            grad_act = grad_act + flat_dot(
                grad_pad[
                    :, 2 - tap_row : 2 - tap_row + row_count, 2 - tap_col : 2 - tap_col + col_count
                ],
                spatial_weight[tap_row, tap_col].T,
            )
    unused, pullback = jax.vjp(activate, clip_wide)
    grad_clip = (cotangent.astype(jnp.float32) + pullback(grad_act)[0]).astype(jnp.bfloat16)
    packed = lax.all_to_all(packed, "height", 0, 0, tiled=True)
    packed = jnp.sum(packed, axis=0)
    packed = packed * grad_scale
    spatial_part = packed[: spatial_rows.shape[1]]
    temporal_part = packed[spatial_rows.shape[1] :]
    return (output, grad_clip, spatial_part, temporal_part)


def solution(mesh):
    return jax.shard_map(
        shards,
        mesh=mesh,
        in_specs=(P("tm", "height", None, None), P("tm", "height", None, None), P(), P()),
        out_specs=(
            P("tm", "height", None, None),
            P("tm", "height", None, None),
            P(("tm", "height")),
            P(("tm", "height")),
        ),
        check_vma=False,
    )
```

```python
import math

import jax
import jax.numpy as jnp
from jax import lax
from jax.sharding import PartitionSpec as P

EPSILON = 1e-06


def extended(cells, sides, width):
    for axis, dim in sides:
        count = lax.axis_size(axis)
        ends = count - 1
        head = lax.slice_in_dim(cells, 0, width, axis=dim)
        tail = lax.slice_in_dim(cells, cells.shape[dim] - width, cells.shape[dim], axis=dim)
        cells = jnp.concatenate(
            [
                lax.ppermute(tail, axis, [(i, (i + 1) % count) for i in range(ends)]),
                cells,
                lax.ppermute(head, axis, [((i + 1) % count, i) for i in range(ends)]),
            ],
            axis=dim,
        )
    return cells


def shifted(block, axis, distance):
    devices = range(lax.axis_size(axis))
    route = [(i - distance, i) for i in devices if i - distance in devices]
    return lax.ppermute(block, axis, route)


def activate(values):
    scale_inv = lax.rsqrt(jnp.mean(values * values, axis=-1, keepdims=True) + EPSILON)
    return jax.nn.silu(values * scale_inv)


def flat_dot(left, weight):
    keep_shape = left.shape[:-1]
    result = jnp.dot(left.reshape(-1, left.shape[-1]), weight, preferred_element_type=jnp.float32)
    return result.reshape(keep_shape + (weight.shape[-1],))


def outer_sum(left, right):
    channels = left.shape[-1]
    return lax.dot_general(
        left.reshape(-1, channels),
        right.reshape(-1, channels),
        (((0,), (0,)), ((), ())),
        preferred_element_type=jnp.float32,
    )


def halving_scatter(block, axis, tie=None, tie_after=0, narrow_from=None):
    count = lax.axis_size(axis)
    index = lax.axis_index(axis)
    step = 1
    while count // step % 2 == 0:
        rest = block.shape[1:]
        pairs = block.reshape((block.shape[0] // 2, 2) + rest)
        mine = index // step % 2
        keep = lax.dynamic_index_in_dim(pairs, mine, axis=1, keepdims=False)
        send = lax.dynamic_index_in_dim(pairs, 1 - mine, axis=1, keepdims=False)
        route = [(i, i ^ step) for i in range(count)]
        if narrow_from is not None and step >= narrow_from:
            sent = lax.ppermute(send.astype(jnp.bfloat16), axis, route).astype(block.dtype)
        else:
            sent = lax.ppermute(send, axis, route)
        block = keep + sent
        if tie is not None and step == 1 << tie_after:
            block, tie = lax.optimization_barrier((block, tie))
        step *= 2
    ways = count // step
    if ways > 1:
        group = index // step
        total = lax.dynamic_index_in_dim(block, group, axis=0, keepdims=True)
        for shift in range(1, ways):
            route = [(i, (i + shift * step) % count) for i in range(count)]
            row = lax.dynamic_index_in_dim(block, (group + shift) % ways, axis=0, keepdims=True)
            total = total + lax.ppermute(row, axis, route)
        block = total
    return block, tie


def shards(clip, cotangent, spatial_weight, temporal_weight):
    frame_count, row_count, col_count, channels = clip.shape
    clip_wide = clip.astype(jnp.float32)
    activated = activate(clip_wide).astype(jnp.bfloat16)
    act_ext = extended(activated, (("height", 1),), 1)
    padded = jnp.pad(act_ext, ((0, 0), (0, 0), (1, 1), (0, 0)))
    spatial = lax.conv_general_dilated(
        padded,
        spatial_weight,
        window_strides=(1, 1),
        padding="VALID",
        dimension_numbers=("NHWC", "HWIO", "NHWC"),
        preferred_element_type=jnp.float32,
    )
    middle = spatial.astype(jnp.bfloat16)
    earlier = shifted(middle, "tm", 1)
    history = jnp.concatenate([earlier, middle], axis=0)
    temporal = jnp.zeros(clip.shape, jnp.float32)
    for time_lag in range(3):
        temporal = temporal + flat_dot(
            history[2 - time_lag : 2 - time_lag + frame_count], temporal_weight[time_lag]
        )
    output = (clip_wide + temporal).astype(jnp.bfloat16)
    later = shifted(cotangent, "tm", -1)
    future = jnp.concatenate([cotangent, later], axis=0)
    grad_wide = jnp.zeros(clip.shape, jnp.float32)
    for time_lag in range(3):
        grad_wide = grad_wide + flat_dot(
            future[time_lag : time_lag + frame_count], temporal_weight[time_lag].T
        )
    grad_mid = grad_wide.astype(jnp.bfloat16)
    grad_temporal = lax.conv_general_dilated(
        history.reshape(history.shape[0], -1, channels),
        cotangent.reshape(frame_count, -1, channels),
        window_strides=(1,),
        padding="VALID",
        dimension_numbers=("WCN", "WIO", "WNC"),
        preferred_element_type=jnp.float32,
    )[::-1]
    grad_spatial = lax.conv_general_dilated(
        padded,
        grad_mid,
        window_strides=(1, 1),
        padding="VALID",
        dimension_numbers=("CHWN", "IHWO", "HWNC"),
        preferred_element_type=jnp.float32,
    ).reshape(9, channels, channels)
    grad_mid_late, unused_history = lax.optimization_barrier((grad_mid, earlier))
    time_shards = lax.axis_size("tm")
    row_shards = lax.axis_size("height")
    grad_scale = 1.0 / math.sqrt(frame_count * time_shards * row_count * row_shards * col_count)
    devices = time_shards * row_shards
    spatial_rows = grad_spatial.reshape(devices, -1)
    temporal_rows = grad_temporal.reshape(devices, -1)
    packed = jnp.concatenate([spatial_rows, temporal_rows], axis=1)
    packed = packed.reshape(time_shards, row_shards, packed.shape[-1])
    packed, grad_mid_late = halving_scatter(packed, "tm", grad_mid_late, 1, narrow_from=2)
    packed = packed[0]
    grad_ext = extended(grad_mid_late, (("height", 1),), 1)
    grad_pad = jnp.pad(grad_ext, ((0, 0), (0, 0), (1, 1), (0, 0)))
    grad_act = jnp.zeros(clip.shape, jnp.float32)
    for tap_row in range(3):
        for tap_col in range(3):
            grad_act = grad_act + flat_dot(
                grad_pad[
                    :, 2 - tap_row : 2 - tap_row + row_count, 2 - tap_col : 2 - tap_col + col_count
                ],
                spatial_weight[tap_row, tap_col].T,
            )
    unused, pullback = jax.vjp(activate, clip_wide)
    grad_clip = (cotangent.astype(jnp.float32) + pullback(grad_act)[0]).astype(jnp.bfloat16)
    packed = lax.all_to_all(packed, "height", 0, 0, tiled=True)
    packed = jnp.sum(packed, axis=0)
    packed = packed * grad_scale
    spatial_part = packed[: spatial_rows.shape[1]]
    temporal_part = packed[spatial_rows.shape[1] :]
    return (output, grad_clip, spatial_part, temporal_part)


def solution(mesh):
    return jax.shard_map(
        shards,
        mesh=mesh,
        in_specs=(P("tm", "height", None, None), P("tm", "height", None, None), P(), P()),
        out_specs=(
            P("tm", "height", None, None),
            P("tm", "height", None, None),
            P(("tm", "height")),
            P(("tm", "height")),
        ),
        check_vma=False,
    )
```

```python
import math

import jax
import jax.numpy as jnp
from jax import lax
from jax.sharding import PartitionSpec as P

EPSILON = 1e-06


def extended(cells, sides, width):
    for axis, dim in sides:
        count = lax.axis_size(axis)
        ends = count - 1
        head = lax.slice_in_dim(cells, 0, width, axis=dim)
        tail = lax.slice_in_dim(cells, cells.shape[dim] - width, cells.shape[dim], axis=dim)
        cells = jnp.concatenate(
            [
                lax.ppermute(tail, axis, [(i, (i + 1) % count) for i in range(ends)]),
                cells,
                lax.ppermute(head, axis, [((i + 1) % count, i) for i in range(ends)]),
            ],
            axis=dim,
        )
    return cells


def shifted(block, axis, distance):
    devices = range(lax.axis_size(axis))
    route = [(i - distance, i) for i in devices if i - distance in devices]
    return lax.ppermute(block, axis, route)


def activate(values):
    scale_inv = lax.rsqrt(jnp.mean(values * values, axis=-1, keepdims=True) + EPSILON)
    return jax.nn.silu(values * scale_inv)


def flat_dot(left, weight):
    keep_shape = left.shape[:-1]
    result = jnp.dot(left.reshape(-1, left.shape[-1]), weight, preferred_element_type=jnp.float32)
    return result.reshape(keep_shape + (weight.shape[-1],))


def outer_sum(left, right):
    channels = left.shape[-1]
    return lax.dot_general(
        left.reshape(-1, channels),
        right.reshape(-1, channels),
        (((0,), (0,)), ((), ())),
        preferred_element_type=jnp.float32,
    )


def halving_scatter(block, axis, tie=None, tie_after=0, narrow_from=None):
    count = lax.axis_size(axis)
    index = lax.axis_index(axis)
    step = 1
    while count // step % 2 == 0:
        rest = block.shape[1:]
        pairs = block.reshape((block.shape[0] // 2, 2) + rest)
        mine = index // step % 2
        keep = lax.dynamic_index_in_dim(pairs, mine, axis=1, keepdims=False)
        send = lax.dynamic_index_in_dim(pairs, 1 - mine, axis=1, keepdims=False)
        route = [(i, i ^ step) for i in range(count)]
        if narrow_from is not None and step >= narrow_from:
            sent = lax.ppermute(send.astype(jnp.bfloat16), axis, route).astype(block.dtype)
        else:
            sent = lax.ppermute(send, axis, route)
        block = keep + sent
        if tie is not None and step == 1 << tie_after:
            block, tie = lax.optimization_barrier((block, tie))
        step *= 2
    ways = count // step
    if ways > 1:
        group = index // step
        total = lax.dynamic_index_in_dim(block, group, axis=0, keepdims=True)
        for shift in range(1, ways):
            route = [(i, (i + shift * step) % count) for i in range(count)]
            row = lax.dynamic_index_in_dim(block, (group + shift) % ways, axis=0, keepdims=True)
            total = total + lax.ppermute(row, axis, route)
        block = total
    return block, tie


def shards(clip, cotangent, spatial_weight, temporal_weight):
    frame_count, row_count, col_count, channels = clip.shape
    clip_wide = clip.astype(jnp.float32)
    activated = activate(clip_wide).astype(jnp.bfloat16)
    act_ext = extended(activated, (("height", 1),), 1)
    padded = jnp.pad(act_ext, ((0, 0), (0, 0), (1, 1), (0, 0)))
    spatial = lax.conv_general_dilated(
        padded,
        spatial_weight,
        window_strides=(1, 1),
        padding="VALID",
        dimension_numbers=("NHWC", "HWIO", "NHWC"),
        preferred_element_type=jnp.float32,
    )
    middle = spatial.astype(jnp.bfloat16)
    earlier = shifted(middle, "tm", 1)
    history = jnp.concatenate([earlier, middle], axis=0)
    temporal = jnp.zeros(clip.shape, jnp.float32)
    for time_lag in range(3):
        temporal = temporal + flat_dot(
            history[2 - time_lag : 2 - time_lag + frame_count], temporal_weight[time_lag]
        )
    output = (clip_wide + temporal).astype(jnp.bfloat16)
    later = shifted(cotangent, "tm", -1)
    future = jnp.concatenate([cotangent, later], axis=0)
    grad_wide = jnp.zeros(clip.shape, jnp.float32)
    for time_lag in range(3):
        grad_wide = grad_wide + flat_dot(
            future[time_lag : time_lag + frame_count], temporal_weight[time_lag].T
        )
    grad_mid = grad_wide.astype(jnp.bfloat16)
    grad_temporal = lax.conv_general_dilated(
        history.reshape(history.shape[0], -1, channels),
        cotangent.reshape(frame_count, -1, channels),
        window_strides=(1,),
        padding="VALID",
        dimension_numbers=("WCN", "WIO", "WNC"),
        preferred_element_type=jnp.float32,
    )[::-1]
    grad_spatial = lax.conv_general_dilated(
        padded,
        grad_mid,
        window_strides=(1, 1),
        padding="VALID",
        dimension_numbers=("CHWN", "IHWO", "HWNC"),
        preferred_element_type=jnp.float32,
    ).reshape(9, channels, channels)
    grad_mid_late, unused_history = lax.optimization_barrier((grad_mid, earlier))
    time_shards = lax.axis_size("tm")
    row_shards = lax.axis_size("height")
    grad_scale = 1.0 / math.sqrt(frame_count * time_shards * row_count * row_shards * col_count)
    devices = time_shards * row_shards
    spatial_rows = grad_spatial.reshape(devices, -1)
    temporal_rows = grad_temporal.reshape(devices, -1)
    packed = jnp.concatenate([spatial_rows, temporal_rows], axis=1)
    packed = packed.reshape(time_shards, row_shards, packed.shape[-1])
    packed, grad_mid_late = halving_scatter(packed, "tm", grad_mid_late, 0, narrow_from=2)
    packed = packed[0]
    grad_ext = extended(grad_mid_late, (("height", 1),), 1)
    grad_pad = jnp.pad(grad_ext, ((0, 0), (0, 0), (1, 1), (0, 0)))
    grad_act = jnp.zeros(clip.shape, jnp.float32)
    for tap_row in range(3):
        for tap_col in range(3):
            grad_act = grad_act + flat_dot(
                grad_pad[
                    :, 2 - tap_row : 2 - tap_row + row_count, 2 - tap_col : 2 - tap_col + col_count
                ],
                spatial_weight[tap_row, tap_col].T,
            )
    unused, pullback = jax.vjp(activate, clip_wide)
    grad_clip = (cotangent.astype(jnp.float32) + pullback(grad_act)[0]).astype(jnp.bfloat16)
    packed = lax.all_to_all(packed, "height", 0, 0, tiled=True)
    packed = jnp.sum(packed, axis=0)
    packed = packed * grad_scale
    spatial_part = packed[: spatial_rows.shape[1]]
    temporal_part = packed[spatial_rows.shape[1] :]
    return (output, grad_clip, spatial_part, temporal_part)


def solution(mesh):
    return jax.shard_map(
        shards,
        mesh=mesh,
        in_specs=(P("tm", "height", None, None), P("tm", "height", None, None), P(), P()),
        out_specs=(
            P("tm", "height", None, None),
            P("tm", "height", None, None),
            P(("tm", "height")),
            P(("tm", "height")),
        ),
        check_vma=False,
    )
```

```python
import math

import jax
import jax.numpy as jnp
from jax import lax
from jax.sharding import PartitionSpec as P

EPSILON = 1e-06


def extended(cells, sides, width):
    for axis, dim in sides:
        count = lax.axis_size(axis)
        ends = count - 1
        head = lax.slice_in_dim(cells, 0, width, axis=dim)
        tail = lax.slice_in_dim(cells, cells.shape[dim] - width, cells.shape[dim], axis=dim)
        cells = jnp.concatenate(
            [
                lax.ppermute(tail, axis, [(i, (i + 1) % count) for i in range(ends)]),
                cells,
                lax.ppermute(head, axis, [((i + 1) % count, i) for i in range(ends)]),
            ],
            axis=dim,
        )
    return cells


def shifted(block, axis, distance):
    devices = range(lax.axis_size(axis))
    route = [(i - distance, i) for i in devices if i - distance in devices]
    return lax.ppermute(block, axis, route)


def activate(values):
    scale_inv = lax.rsqrt(jnp.mean(values * values, axis=-1, keepdims=True) + EPSILON)
    return jax.nn.silu(values * scale_inv)


def flat_dot(left, weight):
    keep_shape = left.shape[:-1]
    result = jnp.dot(left.reshape(-1, left.shape[-1]), weight, preferred_element_type=jnp.float32)
    return result.reshape(keep_shape + (weight.shape[-1],))


def outer_sum(left, right):
    channels = left.shape[-1]
    return lax.dot_general(
        left.reshape(-1, channels),
        right.reshape(-1, channels),
        (((0,), (0,)), ((), ())),
        preferred_element_type=jnp.float32,
    )


def halving_scatter(block, axis, tie=None, tie_after=0, narrow_from=None):
    count = lax.axis_size(axis)
    index = lax.axis_index(axis)
    step = 1
    while count // step % 2 == 0:
        rest = block.shape[1:]
        pairs = block.reshape((block.shape[0] // 2, 2) + rest)
        mine = index // step % 2
        keep = lax.dynamic_index_in_dim(pairs, mine, axis=1, keepdims=False)
        send = lax.dynamic_index_in_dim(pairs, 1 - mine, axis=1, keepdims=False)
        route = [(i, i ^ step) for i in range(count)]
        if narrow_from is not None and step >= narrow_from:
            sent = lax.ppermute(send.astype(jnp.bfloat16), axis, route).astype(block.dtype)
        else:
            sent = lax.ppermute(send, axis, route)
        block = keep + sent
        if tie is not None and step == 1 << tie_after:
            block, tie = lax.optimization_barrier((block, tie))
        step *= 2
    ways = count // step
    if ways > 1:
        group = index // step
        total = lax.dynamic_index_in_dim(block, group, axis=0, keepdims=True)
        for shift in range(1, ways):
            route = [(i, (i + shift * step) % count) for i in range(count)]
            row = lax.dynamic_index_in_dim(block, (group + shift) % ways, axis=0, keepdims=True)
            total = total + lax.ppermute(row, axis, route)
        block = total
    return block, tie


def shards(clip, cotangent, spatial_weight, temporal_weight):
    frame_count, row_count, col_count, channels = clip.shape
    clip_wide = clip.astype(jnp.float32)
    activated = activate(clip_wide).astype(jnp.bfloat16)
    act_ext = extended(activated, (("height", 1),), 1)
    padded = jnp.pad(act_ext, ((0, 0), (0, 0), (1, 1), (0, 0)))
    spatial = lax.conv_general_dilated(
        padded,
        spatial_weight,
        window_strides=(1, 1),
        padding="VALID",
        dimension_numbers=("NHWC", "HWIO", "NHWC"),
        preferred_element_type=jnp.float32,
    )
    middle = spatial.astype(jnp.bfloat16)
    earlier = shifted(middle, "tm", 1)
    history = jnp.concatenate([earlier, middle], axis=0)
    temporal = jnp.zeros(clip.shape, jnp.float32)
    for time_lag in range(3):
        temporal = temporal + flat_dot(
            history[2 - time_lag : 2 - time_lag + frame_count], temporal_weight[time_lag]
        )
    output = (clip_wide + temporal).astype(jnp.bfloat16)
    later = shifted(cotangent, "tm", -1)
    future = jnp.concatenate([cotangent, later], axis=0)
    grad_wide = jnp.zeros(clip.shape, jnp.float32)
    for time_lag in range(3):
        grad_wide = grad_wide + flat_dot(
            future[time_lag : time_lag + frame_count], temporal_weight[time_lag].T
        )
    grad_mid = grad_wide.astype(jnp.bfloat16)
    grad_temporal = lax.conv_general_dilated(
        history.reshape(history.shape[0], -1, channels),
        cotangent.reshape(frame_count, -1, channels),
        window_strides=(1,),
        padding="VALID",
        dimension_numbers=("WCN", "WIO", "WNC"),
        preferred_element_type=jnp.float32,
    )[::-1]
    grad_spatial = lax.conv_general_dilated(
        padded,
        grad_mid,
        window_strides=(1, 1),
        padding="VALID",
        dimension_numbers=("CHWN", "IHWO", "HWNC"),
        preferred_element_type=jnp.float32,
    ).reshape(9, channels, channels)
    grad_mid_late, unused_history = lax.optimization_barrier((grad_mid, earlier))
    time_shards = lax.axis_size("tm")
    row_shards = lax.axis_size("height")
    grad_scale = 1.0 / math.sqrt(frame_count * time_shards * row_count * row_shards * col_count)
    devices = time_shards * row_shards
    spatial_rows = grad_spatial.reshape(devices, -1)
    temporal_rows = grad_temporal.reshape(devices, -1)
    packed = jnp.concatenate([spatial_rows, temporal_rows], axis=1)
    packed = packed.reshape(time_shards, row_shards, packed.shape[-1])
    packed, grad_mid_late = halving_scatter(packed, "tm", grad_mid_late, 0, narrow_from=2)
    packed = packed[0]
    grad_ext = extended(grad_mid_late, (("height", 1),), 1)
    grad_pad = jnp.pad(grad_ext, ((0, 0), (0, 0), (1, 1), (0, 0)))
    grad_act = lax.conv_general_dilated(
        grad_pad,
        jnp.swapaxes(spatial_weight[::-1, ::-1], 2, 3),
        window_strides=(1, 1),
        padding="VALID",
        dimension_numbers=("NHWC", "HWIO", "NHWC"),
        preferred_element_type=jnp.float32,
    )
    unused, pullback = jax.vjp(activate, clip_wide)
    grad_clip = (cotangent.astype(jnp.float32) + pullback(grad_act)[0]).astype(jnp.bfloat16)
    packed = lax.all_to_all(packed, "height", 0, 0, tiled=True)
    packed = jnp.sum(packed, axis=0)
    packed = packed * grad_scale
    spatial_part = packed[: spatial_rows.shape[1]]
    temporal_part = packed[spatial_rows.shape[1] :]
    return (output, grad_clip, spatial_part, temporal_part)


def solution(mesh):
    return jax.shard_map(
        shards,
        mesh=mesh,
        in_specs=(P("tm", "height", None, None), P("tm", "height", None, None), P(), P()),
        out_specs=(
            P("tm", "height", None, None),
            P("tm", "height", None, None),
            P(("tm", "height")),
            P(("tm", "height")),
        ),
        check_vma=False,
    )
```

```python
import math

import jax
import jax.numpy as jnp
from jax import lax
from jax.sharding import PartitionSpec as P

EPSILON = 1e-06


def extended(cells, sides, width):
    for axis, dim in sides:
        count = lax.axis_size(axis)
        ends = count - 1
        head = lax.slice_in_dim(cells, 0, width, axis=dim)
        tail = lax.slice_in_dim(cells, cells.shape[dim] - width, cells.shape[dim], axis=dim)
        cells = jnp.concatenate(
            [
                lax.ppermute(tail, axis, [(i, (i + 1) % count) for i in range(ends)]),
                cells,
                lax.ppermute(head, axis, [((i + 1) % count, i) for i in range(ends)]),
            ],
            axis=dim,
        )
    return cells


def shifted(block, axis, distance):
    devices = range(lax.axis_size(axis))
    route = [(i - distance, i) for i in devices if i - distance in devices]
    return lax.ppermute(block, axis, route)


def activate(values):
    scale_inv = lax.rsqrt(jnp.mean(values * values, axis=-1, keepdims=True) + EPSILON)
    return jax.nn.silu(values * scale_inv)


def flat_dot(left, weight):
    keep_shape = left.shape[:-1]
    result = jnp.dot(left.reshape(-1, left.shape[-1]), weight, preferred_element_type=jnp.float32)
    return result.reshape(keep_shape + (weight.shape[-1],))


def outer_sum(left, right):
    channels = left.shape[-1]
    return lax.dot_general(
        left.reshape(-1, channels),
        right.reshape(-1, channels),
        (((0,), (0,)), ((), ())),
        preferred_element_type=jnp.float32,
    )


def halving_scatter(block, axis, tie=None, tie_after=0, narrow_from=None):
    count = lax.axis_size(axis)
    index = lax.axis_index(axis)
    step = 1
    while count // step % 2 == 0:
        rest = block.shape[1:]
        pairs = block.reshape((block.shape[0] // 2, 2) + rest)
        mine = index // step % 2
        keep = lax.dynamic_index_in_dim(pairs, mine, axis=1, keepdims=False)
        send = lax.dynamic_index_in_dim(pairs, 1 - mine, axis=1, keepdims=False)
        route = [(i, i ^ step) for i in range(count)]
        if narrow_from is not None and step >= narrow_from:
            sent = lax.ppermute(send.astype(jnp.bfloat16), axis, route).astype(block.dtype)
        else:
            sent = lax.ppermute(send, axis, route)
        block = keep + sent
        if tie is not None and step == 1 << tie_after:
            block, tie = lax.optimization_barrier((block, tie))
        step *= 2
    ways = count // step
    if ways > 1:
        group = index // step
        total = lax.dynamic_index_in_dim(block, group, axis=0, keepdims=True)
        for shift in range(1, ways):
            route = [(i, (i + shift * step) % count) for i in range(count)]
            row = lax.dynamic_index_in_dim(block, (group + shift) % ways, axis=0, keepdims=True)
            total = total + lax.ppermute(row, axis, route)
        block = total
    return block, tie


def shards(clip, cotangent, spatial_weight, temporal_weight):
    frame_count, row_count, col_count, channels = clip.shape
    clip_wide = clip.astype(jnp.float32)
    activated = activate(clip_wide).astype(jnp.bfloat16)
    act_ext = extended(activated, (("height", 1),), 1)
    padded = jnp.pad(act_ext, ((0, 0), (0, 0), (1, 1), (0, 0)))
    spatial = lax.conv_general_dilated(
        padded,
        spatial_weight,
        window_strides=(1, 1),
        padding="VALID",
        dimension_numbers=("NHWC", "HWIO", "NHWC"),
        preferred_element_type=jnp.float32,
    )
    middle = spatial.astype(jnp.bfloat16)
    earlier = shifted(middle, "tm", 1)
    history = jnp.concatenate([earlier, middle], axis=0)
    temporal = jnp.zeros(clip.shape, jnp.float32)
    for time_lag in range(3):
        temporal = temporal + flat_dot(
            history[2 - time_lag : 2 - time_lag + frame_count], temporal_weight[time_lag]
        )
    output = (clip_wide + temporal).astype(jnp.bfloat16)
    later = shifted(cotangent, "tm", -1)
    future = jnp.concatenate([cotangent, later], axis=0)
    grad_wide = jnp.zeros(clip.shape, jnp.float32)
    for time_lag in range(3):
        grad_wide = grad_wide + flat_dot(
            future[time_lag : time_lag + frame_count], temporal_weight[time_lag].T
        )
    grad_mid = grad_wide.astype(jnp.bfloat16)
    grad_temporal = lax.conv_general_dilated(
        history[::-1].reshape(history.shape[0], -1, channels),
        cotangent[::-1].reshape(frame_count, -1, channels),
        window_strides=(1,),
        padding="VALID",
        dimension_numbers=("WCN", "WIO", "WNC"),
        preferred_element_type=jnp.float32,
    )
    grad_spatial = lax.conv_general_dilated(
        padded,
        grad_mid,
        window_strides=(1, 1),
        padding="VALID",
        dimension_numbers=("CHWN", "IHWO", "HWNC"),
        preferred_element_type=jnp.float32,
    ).reshape(9, channels, channels)
    grad_mid_late, unused_history = lax.optimization_barrier((grad_mid, earlier))
    time_shards = lax.axis_size("tm")
    row_shards = lax.axis_size("height")
    grad_scale = 1.0 / math.sqrt(frame_count * time_shards * row_count * row_shards * col_count)
    devices = time_shards * row_shards
    spatial_rows = grad_spatial.reshape(devices, -1)
    temporal_rows = grad_temporal.reshape(devices, -1)
    packed = jnp.concatenate([spatial_rows, temporal_rows], axis=1)
    packed = packed.reshape(time_shards, row_shards, packed.shape[-1])
    packed, grad_mid_late = halving_scatter(packed, "tm", grad_mid_late, 0, narrow_from=2)
    packed = packed[0]
    grad_ext = extended(grad_mid_late, (("height", 1),), 1)
    grad_pad = jnp.pad(grad_ext, ((0, 0), (0, 0), (1, 1), (0, 0)))
    grad_act = lax.conv_general_dilated(
        grad_pad,
        jnp.swapaxes(spatial_weight[::-1, ::-1], 2, 3),
        window_strides=(1, 1),
        padding="VALID",
        dimension_numbers=("NHWC", "HWIO", "NHWC"),
        preferred_element_type=jnp.float32,
    )
    unused, pullback = jax.vjp(activate, clip_wide)
    grad_clip = (cotangent.astype(jnp.float32) + pullback(grad_act)[0]).astype(jnp.bfloat16)
    packed = lax.all_to_all(packed, "height", 0, 0, tiled=True)
    packed = jnp.sum(packed, axis=0)
    packed = packed * grad_scale
    spatial_part = packed[: spatial_rows.shape[1]]
    temporal_part = packed[spatial_rows.shape[1] :]
    return (output, grad_clip, spatial_part, temporal_part)


def solution(mesh):
    return jax.shard_map(
        shards,
        mesh=mesh,
        in_specs=(P("tm", "height", None, None), P("tm", "height", None, None), P(), P()),
        out_specs=(
            P("tm", "height", None, None),
            P("tm", "height", None, None),
            P(("tm", "height")),
            P(("tm", "height")),
        ),
        check_vma=False,
    )
```
